128 devices in a mesh: sample: 8 (over x, y_hi), landmark: 16 (over z, y_lo, core).
Axes of the slice: x: 4, y: 4 (y_hi: 2, y_lo: 2; y = y_hi * 2 + y_lo), z: 4, core: 2. Of those that a mesh axis runs over, the one named last changes fastest.
Arguments:
- summaries: bfloat16 [16384, 1024], P('sample', 'landmark'), may hold values from -12 to 12
- row_level: int32 [16384], P('sample'), may hold values from 0 to 3
- pool: bfloat16 [32768, 1024], P('landmark'), may hold values from -6 to 6
- pool_level: int32 [32768], P('landmark'), may hold values from 0 to 3
- landmark_index: int32 [16384], P('landmark'), may hold values from 0 to 2047, as said below
- level_scale: float32 [4], replicated, may hold values from 1.2 to 2.4
- targets: bfloat16 [16384, 256], P('sample'), may hold values from -6 to 6
Outputs:
- weights: float32 [16384, 256], P('landmark')
- residual: float32 [16384, 256], P('landmark')
The draws below stay inside these ranges and needn't reach their ends.
Inputs may be any that keep to these rules, and one draw needn't show every extreme that they name: Landmark j is pool row (j // 1024) * 2048 + landmark_index[j], a row of the pool block of its own landmark group; indices may repeat.
All inputs are finite; a program needn't handle non-finite values.
Results may differ from the reference program's by a relative error of at most 0.012.
Values may be sent and summed in bfloat16 or wider, within the bound.
No kernel may reach another device: no remote copies, remote signals or barrier semaphores. Data moves between devices by JAX's collectives and lax.ppermute only.
A program may use at most 64 MiB of HBM per device.

```python
import math
import jax
import jax.numpy as jnp
from jax import lax

F = 1024
P_SIZE = 256
M_DEV = 1024
ROWS_DEV = 2048
LEVELS = 4
ITERS = 2
POOL_DEV = 2048
ROWS = 16384
M = 16384
POOL = 32768
N_SAMPLE = 8
N_LANDMARK = 16


def draw_landmark_index(key, part):
    chosen = jax.random.randint(key, (M,), 0, POOL_DEV, dtype=jnp.int32)
    position = jnp.arange(M, dtype=jnp.int32) % M_DEV
    chosen = jnp.where(position == 0, jnp.zeros_like(chosen), chosen)
    chosen = jnp.where(position == 1, jnp.full_like(chosen, POOL_DEV - 1), chosen)
    return chosen


def draw_summaries(key, part):
    noise_key = jax.random.fold_in(key, 11)
    common_key = jax.random.fold_in(key, 12)
    common = jnp.clip(jax.random.normal(common_key, (F,), jnp.float32), -2.5, 2.5) * F ** (-0.25)
    position = jnp.arange(ROWS, dtype=jnp.float32) / max(ROWS - 1, 1)
    noise = jnp.clip(jax.random.normal(noise_key, (ROWS, F), jnp.float32), -6.0, 6.0)
    ramp = 1.5 * position
    values = noise + ramp[:, None] * common[None, :]
    return jnp.clip(values, -12.0, 12.0).astype(jnp.bfloat16)


def set_ends(drawn, own_key, low, largest):
    extent = drawn.shape
    place = [jax.random.randint(jax.random.fold_in(own_key, axis), (), 0, extent[axis]) for axis in range(len(extent))]
    drawn = drawn.at[tuple(place)].set(low)
    longest = extent.index(max(extent))
    place[longest] = (place[longest] + 1) % extent[longest]
    return drawn.at[tuple(place)].set(largest)


def level_of(own_key, dims, split, smallest, high):
    def one(dim, shards_of):
        steps = jax.random.uniform(jax.random.fold_in(jax.random.fold_in(own_key, 6), dim), (shards_of,), jnp.float32, smallest / len(split), high / len(split))
        return jnp.repeat(jnp.exp(steps), dims[dim] // shards_of).reshape((-1,) + (1,) * (len(dims) - dim - 1))

    loudness = one(*split[0])
    for cut in split[1:]:
        loudness = loudness * one(*cut)
    return loudness


def bell_draw(own_key, shape, scale, reach, pieces=(), kind=jnp.bfloat16):
    values = jax.random.normal(own_key, shape, jnp.float32) * scale
    if len(pieces) > 0:
        values = level_of(own_key, shape, pieces, -0.22, 0.18) * values
    return jnp.clip(values, min=-reach, max=reach).astype(kind)


def setup_inputs(seed: int = 0) -> dict:
    keys = jax.random.split(jax.random.key(seed), 8)
    return {
        "summaries": draw_summaries(jax.random.fold_in(keys[7], 71), 0),
        "row_level": set_ends(jax.random.randint(keys[1], (ROWS,), 0, LEVELS), jax.random.fold_in(keys[1], 1), 0, LEVELS - 1).astype(jnp.int32),
        "pool": bell_draw(keys[2], (POOL, F), 1.0, 6.0, ((0, 16),)),
        "pool_level": set_ends(jax.random.randint(keys[3], (POOL,), 0, LEVELS), jax.random.fold_in(keys[3], 1), 0, LEVELS - 1).astype(jnp.int32),
        "landmark_index": draw_landmark_index(jax.random.fold_in(keys[7], 71), 0),
        "level_scale": jnp.clip(jnp.exp(jax.random.uniform(keys[5], (LEVELS,), jnp.float32, math.log(1.2), math.log(2.4))), 1.2, 2.4),
        "targets": bell_draw(keys[6], (ROWS, P_SIZE), 1.0, 6.0, ((0, 8),)),
    }


ridge = 0.5

def level_values(level_ids, level_table):
    onehot = level_ids[:, None] == jnp.arange(level_table.shape[0], dtype=jnp.int32)[None, :]
    return lax.optimization_barrier(jnp.sum(jnp.where(onehot, level_table[None, :], jnp.zeros_like(level_table)[None, :]), axis=1))

def raw_block(summary_rows, row_factor, anchors, anchor_factor):
    scores = jnp.dot(summary_rows, anchors.T, preferred_element_type=jnp.float32)
    return jnp.exp(scores * row_factor[:, None] * anchor_factor[None, :])

def kernel_block(summary_rows, row_factor, anchors, anchor_factor, column_mean):
    raw = raw_block(summary_rows, row_factor, anchors, anchor_factor)
    return (raw - column_mean[None, :]).astype(jnp.bfloat16)

def reference(summaries, row_level, pool, pool_level, landmark_index, level_scale, targets):
    n_rows = ROWS_DEV * N_SAMPLE
    feature_count = summaries.shape[1]
    column_count = targets.shape[1]
    offsets = jnp.arange(M_DEV * N_LANDMARK, dtype=jnp.int32) // M_DEV * POOL_DEV
    chosen = (landmark_index + offsets).astype(jnp.int32)
    anchors = jnp.take(pool, chosen, axis=0)
    anchor_level = jnp.take(pool_level, chosen, axis=0)
    row_factor = 1.0 / math.sqrt(feature_count) / level_values(row_level, level_scale)
    anchor_factor = 1.0 / level_values(anchor_level, level_scale)
    anchor_blocks = anchors.reshape(N_LANDMARK, M_DEV, feature_count)
    factor_blocks = anchor_factor.reshape(N_LANDMARK, M_DEV)

    def mean_block(pair):
        return lax.optimization_barrier(jnp.sum(raw_block(summaries, row_factor, pair[0], pair[1]), axis=0)) / n_rows
    mean_blocks = lax.map(mean_block, (anchor_blocks, factor_blocks))

    def rhs_block(triple):
        kernel = kernel_block(summaries, row_factor, triple[0], triple[1], triple[2])
        return jnp.dot(kernel.T, targets, preferred_element_type=jnp.float32)
    rhs = lax.map(rhs_block, (anchor_blocks, factor_blocks, mean_blocks)).reshape(-1, column_count) / math.sqrt(n_rows)

    def apply(direction):
        direction_half = direction.astype(jnp.bfloat16).reshape(N_LANDMARK, M_DEV, column_count)

        def accumulate(total, quad):
            kernel = kernel_block(summaries, row_factor, quad[0], quad[1], quad[2])
            return (total + jnp.dot(kernel, quad[3], preferred_element_type=jnp.float32), None)
        scanned = lax.scan(accumulate, jnp.zeros((n_rows, column_count), jnp.float32), (anchor_blocks, factor_blocks, mean_blocks, direction_half))
        row_half = scanned[0].astype(jnp.bfloat16)

        def back_block(triple):
            kernel = kernel_block(summaries, row_factor, triple[0], triple[1], triple[2])
            return jnp.dot(kernel.T, row_half, preferred_element_type=jnp.float32)
        column_part = lax.map(back_block, (anchor_blocks, factor_blocks, mean_blocks)).reshape(-1, column_count)
        return column_part / n_rows + ridge * direction
    weights = jnp.zeros_like(rhs)
    residual = rhs
    direction = rhs
    norm_now = lax.optimization_barrier(jnp.sum(residual * residual, axis=0))
    for iteration in range(ITERS):
        image = apply(direction)
        step_size = norm_now / lax.optimization_barrier(jnp.sum(direction * image, axis=0))
        weights = weights + step_size * direction
        residual = residual - step_size * image
        norm_next = lax.optimization_barrier(jnp.sum(residual * residual, axis=0))
        direction = residual + norm_next / norm_now * direction
        norm_now = norm_next
    return (weights, residual)
```

```python
import math

import jax
import jax.numpy as jnp
from jax import lax
from jax.sharding import PartitionSpec as P

ITERS = 2


ridge = 0.5


def level_values(level_ids, level_table):
    onehot = level_ids[:, None] == jnp.arange(level_table.shape[0], dtype=jnp.int32)[None, :]
    return jnp.sum(
        jnp.where(onehot, level_table[None, :], jnp.zeros_like(level_table)[None, :]), axis=1
    )


def raw_block(summary_rows, row_factor, anchors, anchor_factor):
    scores = jnp.dot(summary_rows, anchors.T, preferred_element_type=jnp.float32)
    return jnp.exp(scores * row_factor[:, None] * anchor_factor[None, :])


def partner_bits(size, order):
    bits = [b for b in order if b < size]
    assert sorted(bits) == [1 << i for i in range(size.bit_length() - 1)]
    return bits


def butterfly_sum(x, axis, bits):
    size = lax.axis_size(axis)
    for k in bits:
        perm = [(i, i ^ k) for i in range(size)]
        x = x + lax.ppermute(x, axis, perm)
    return x


def halving_sum(x, extra, axis, bits, gather_dtype):
    size = lax.axis_size(axis)
    index = lax.axis_index(axis)
    for k in bits:
        perm = [(i, i ^ k) for i in range(size)]
        half = x.shape[0] // 2
        mine = (index // k) % 2
        keep = lax.dynamic_slice_in_dim(x, mine * half, half, axis=0)
        send = lax.dynamic_slice_in_dim(x, (1 - mine) * half, half, axis=0)
        got, got_extra = lax.ppermute((send, extra), axis, perm)
        x = keep + got
        extra = extra + got_extra
    x = x.astype(gather_dtype)
    for k in reversed(bits):
        perm = [(i, i ^ k) for i in range(size)]
        part = x.shape[0]
        mine = (index // k) % 2
        got = lax.ppermute(x, axis, perm)
        whole = jnp.zeros((2 * part,) + x.shape[1:], x.dtype)
        whole = lax.dynamic_update_slice_in_dim(whole, x, mine * part, axis=0)
        x = lax.dynamic_update_slice_in_dim(whole, got, (1 - mine) * part, axis=0)
    return x, extra


def on_device(summaries, row_level, pool, pool_level, landmark_index, level_scale, targets):
    sample_bits = partner_bits(lax.axis_size("sample"), (2, 1, 4, 8, 16, 32, 64))
    landmark_bits = partner_bits(lax.axis_size("landmark"), (1, 2, 4, 8, 16, 32, 64))
    row_count = summaries.shape[0]
    n_rows = row_count * lax.axis_size("sample")
    gathered = lax.all_gather(summaries, "landmark", axis=1, tiled=True)
    feature_count = gathered.shape[1]
    anchors = jnp.take(pool, landmark_index, axis=0)
    anchor_level = jnp.take(pool_level, landmark_index, axis=0)
    row_factor = 1.0 / math.sqrt(feature_count) / level_values(row_level, level_scale)
    anchor_factor = 1.0 / level_values(anchor_level, level_scale)
    raw = raw_block(gathered, row_factor, anchors, anchor_factor)
    column_mean = butterfly_sum(jnp.sum(raw, axis=0), "sample", sample_bits) / n_rows
    kernel = (raw - column_mean[None, :]).astype(jnp.bfloat16)
    rhs_part = jnp.dot(kernel.T, targets, preferred_element_type=jnp.float32)
    rhs_total, _ = halving_sum(rhs_part, jnp.zeros((1,), jnp.float32), "sample", sample_bits, jnp.float32)
    rhs = rhs_total / math.sqrt(n_rows)
    weights = jnp.zeros_like(rhs)
    residual = rhs
    direction = rhs
    norm_now = None
    for iteration in range(ITERS):
        direction_half = direction.astype(jnp.bfloat16)
        row_part = jnp.dot(kernel, direction_half, preferred_element_type=jnp.float32)
        sums = [jnp.sum(direction * direction, axis=0)]
        if norm_now is None:
            sums.append(jnp.sum(residual * residual, axis=0))
        row_half, landmark_sums = halving_sum(
            row_part, jnp.concatenate(sums), "landmark", landmark_bits, jnp.bfloat16
        )
        column_count = direction.shape[1]
        direction_square = landmark_sums[:column_count]
        if norm_now is None:
            norm_now = landmark_sums[column_count:]
        row_square = jnp.sum(jnp.square(row_half.astype(jnp.float32)), axis=0)
        column_part = jnp.dot(kernel.T, row_half, preferred_element_type=jnp.float32)
        column_total, row_square_total = halving_sum(
            column_part, row_square, "sample", sample_bits, jnp.float32
        )
        image = column_total / n_rows + ridge * direction
        curvature = row_square_total / n_rows + ridge * direction_square
        step_size = norm_now / curvature
        weights = weights + step_size * direction
        residual = residual - step_size * image
        norm_next = butterfly_sum(jnp.sum(residual * residual, axis=0), "landmark", landmark_bits)
        direction = residual + norm_next / norm_now * direction
        norm_now = norm_next
    return (weights, residual)


def solution(mesh):
    return jax.shard_map(
        on_device,
        mesh=mesh,
        in_specs=(
            P("sample", "landmark"),
            P("sample"),
            P("landmark", None),
            P("landmark"),
            P("landmark"),
            P(),
            P("sample", None),
        ),
        out_specs=(P("landmark", None), P("landmark", None)),
        check_vma=False,
    )
```

```python
import math

import jax
import jax.numpy as jnp
from jax import lax
from jax.sharding import PartitionSpec as P

ITERS = 2


ridge = 0.5


def level_values(level_ids, level_table):
    onehot = level_ids[:, None] == jnp.arange(level_table.shape[0], dtype=jnp.int32)[None, :]
    return jnp.sum(
        jnp.where(onehot, level_table[None, :], jnp.zeros_like(level_table)[None, :]), axis=1
    )


def raw_block(summary_rows, row_factor, anchors, anchor_factor):
    scores = jnp.dot(summary_rows, anchors.T, preferred_element_type=jnp.float32)
    return jnp.exp(scores * row_factor[:, None] * anchor_factor[None, :])


def partner_bits(size, order):
    bits = [b for b in order if b < size]
    assert sorted(bits) == [1 << i for i in range(size.bit_length() - 1)]
    return bits


def butterfly_sum(x, axis, bits):
    size = lax.axis_size(axis)
    for k in bits:
        perm = [(i, i ^ k) for i in range(size)]
        x = x + lax.ppermute(x, axis, perm)
    return x


def halving_sum(x, extra, axis, bits, gather_dtype, wire_dtype=jnp.bfloat16):
    size = lax.axis_size(axis)
    index = lax.axis_index(axis)
    for k in bits:
        perm = [(i, i ^ k) for i in range(size)]
        half = x.shape[0] // 2
        mine = (index // k) % 2
        keep = lax.dynamic_slice_in_dim(x, mine * half, half, axis=0)
        send = lax.dynamic_slice_in_dim(x, (1 - mine) * half, half, axis=0)
        got, got_extra = lax.ppermute((send.astype(wire_dtype), extra), axis, perm)
        x = keep + got.astype(jnp.float32)
        extra = extra + got_extra
    x = x.astype(gather_dtype)
    for k in reversed(bits):
        perm = [(i, i ^ k) for i in range(size)]
        part = x.shape[0]
        mine = (index // k) % 2
        got = lax.ppermute(x, axis, perm)
        whole = jnp.zeros((2 * part,) + x.shape[1:], x.dtype)
        whole = lax.dynamic_update_slice_in_dim(whole, x, mine * part, axis=0)
        x = lax.dynamic_update_slice_in_dim(whole, got, (1 - mine) * part, axis=0)
    return x, extra


def on_device(summaries, row_level, pool, pool_level, landmark_index, level_scale, targets):
    sample_bits = partner_bits(lax.axis_size("sample"), (2, 1, 4, 8, 16, 32, 64))
    landmark_bits = partner_bits(lax.axis_size("landmark"), (1, 2, 4, 8, 16, 32, 64))
    row_count = summaries.shape[0]
    n_rows = row_count * lax.axis_size("sample")
    gathered = lax.all_gather(summaries, "landmark", axis=1, tiled=True)
    feature_count = gathered.shape[1]
    anchors = jnp.take(pool, landmark_index, axis=0)
    anchor_level = jnp.take(pool_level, landmark_index, axis=0)
    row_factor = 1.0 / math.sqrt(feature_count) / level_values(row_level, level_scale)
    anchor_factor = 1.0 / level_values(anchor_level, level_scale)
    raw = raw_block(gathered, row_factor, anchors, anchor_factor)
    column_mean = butterfly_sum(jnp.sum(raw, axis=0), "sample", sample_bits) / n_rows
    kernel = (raw - column_mean[None, :]).astype(jnp.bfloat16)
    rhs_part = jnp.dot(kernel.T, targets, preferred_element_type=jnp.float32)
    rhs_total, _ = halving_sum(rhs_part, jnp.zeros((1,), jnp.float32), "sample", sample_bits, jnp.float32)
    rhs = rhs_total / math.sqrt(n_rows)
    weights = jnp.zeros_like(rhs)
    residual = rhs
    direction = rhs
    norm_now = None
    for iteration in range(ITERS):
        direction_half = direction.astype(jnp.bfloat16)
        row_part = jnp.dot(kernel, direction_half, preferred_element_type=jnp.float32)
        sums = [jnp.sum(direction * direction, axis=0)]
        if norm_now is None:
            sums.append(jnp.sum(residual * residual, axis=0))
        row_half, landmark_sums = halving_sum(
            row_part, jnp.concatenate(sums), "landmark", landmark_bits, jnp.bfloat16
        )
        column_count = direction.shape[1]
        direction_square = landmark_sums[:column_count]
        if norm_now is None:
            norm_now = landmark_sums[column_count:]
        row_square = jnp.sum(jnp.square(row_half.astype(jnp.float32)), axis=0)
        column_part = jnp.dot(kernel.T, row_half, preferred_element_type=jnp.float32)
        column_total, row_square_total = halving_sum(
            column_part, row_square, "sample", sample_bits, jnp.float32
        )
        image = column_total / n_rows + ridge * direction
        curvature = row_square_total / n_rows + ridge * direction_square
        step_size = norm_now / curvature
        weights = weights + step_size * direction
        residual = residual - step_size * image
        norm_next = butterfly_sum(jnp.sum(residual * residual, axis=0), "landmark", landmark_bits)
        direction = residual + norm_next / norm_now * direction
        norm_now = norm_next
    return (weights, residual)


def solution(mesh):
    return jax.shard_map(
        on_device,
        mesh=mesh,
        in_specs=(
            P("sample", "landmark"),
            P("sample"),
            P("landmark", None),
            P("landmark"),
            P("landmark"),
            P(),
            P("sample", None),
        ),
        out_specs=(P("landmark", None), P("landmark", None)),
        check_vma=False,
    )
```

```python
import math

import jax
import jax.numpy as jnp
from jax import lax
from jax.sharding import PartitionSpec as P

ITERS = 2


ridge = 0.5


def level_values(level_ids, level_table):
    onehot = level_ids[:, None] == jnp.arange(level_table.shape[0], dtype=jnp.int32)[None, :]
    return jnp.sum(
        jnp.where(onehot, level_table[None, :], jnp.zeros_like(level_table)[None, :]), axis=1
    )


def raw_block(summary_rows, row_factor, anchors, anchor_factor):
    scores = jnp.dot(summary_rows, anchors.T, preferred_element_type=jnp.float32)
    return jnp.exp(scores * row_factor[:, None] * anchor_factor[None, :])


def partner_bits(size, order):
    bits = [b for b in order if b < size]
    assert sorted(bits) == [1 << i for i in range(size.bit_length() - 1)]
    return bits


def butterfly_sum(x, axis, bits):
    size = lax.axis_size(axis)
    for k in bits:
        perm = [(i, i ^ k) for i in range(size)]
        x = x + lax.ppermute(x, axis, perm)
    return x


def halving_sum(x, extra, axis, bits, gather_dtype, wire_dtype=jnp.bfloat16):
    size = lax.axis_size(axis)
    index = lax.axis_index(axis)
    for k in bits:
        perm = [(i, i ^ k) for i in range(size)]
        half = x.shape[0] // 2
        mine = (index // k) % 2
        keep = lax.dynamic_slice_in_dim(x, mine * half, half, axis=0)
        send = lax.dynamic_slice_in_dim(x, (1 - mine) * half, half, axis=0)
        got, got_extra = lax.ppermute((send.astype(wire_dtype), extra), axis, perm)
        x = keep + got.astype(jnp.float32)
        extra = extra + got_extra
    x = x.astype(gather_dtype)
    for k in reversed(bits):
        perm = [(i, i ^ k) for i in range(size)]
        part = x.shape[0]
        mine = (index // k) % 2
        got = lax.ppermute(x, axis, perm)
        whole = jnp.zeros((2 * part,) + x.shape[1:], x.dtype)
        whole = lax.dynamic_update_slice_in_dim(whole, x, mine * part, axis=0)
        x = lax.dynamic_update_slice_in_dim(whole, got, (1 - mine) * part, axis=0)
    return x, extra


def on_device(summaries, row_level, pool, pool_level, landmark_index, level_scale, targets):
    sample_bits = partner_bits(lax.axis_size("sample"), (2, 1, 4, 8, 16, 32, 64))
    landmark_bits = partner_bits(lax.axis_size("landmark"), (1, 2, 4, 8, 16, 32, 64))
    row_count = summaries.shape[0]
    n_rows = row_count * lax.axis_size("sample")
    gathered = lax.all_gather(summaries, "landmark", axis=1, tiled=True)
    feature_count = gathered.shape[1]
    anchors = jnp.take(pool, landmark_index, axis=0)
    anchor_level = jnp.take(pool_level, landmark_index, axis=0)
    row_factor = 1.0 / math.sqrt(feature_count) / level_values(row_level, level_scale)
    anchor_factor = 1.0 / level_values(anchor_level, level_scale)
    raw = raw_block(gathered, row_factor, anchors, anchor_factor)
    column_mean = butterfly_sum(jnp.sum(raw, axis=0), "sample", sample_bits) / n_rows
    kernel = (raw - column_mean[None, :]).astype(jnp.bfloat16)
    rhs_part = jnp.dot(kernel.T, targets, preferred_element_type=jnp.float32)
    rhs_total, _ = halving_sum(
        rhs_part, jnp.zeros((1,), jnp.float32), "sample", sample_bits, jnp.float32, jnp.float32
    )
    rhs = rhs_total / math.sqrt(n_rows)
    weights = jnp.zeros_like(rhs)
    residual = rhs
    direction = rhs
    norm_now = None
    for iteration in range(ITERS):
        direction_half = direction.astype(jnp.bfloat16)
        row_part = jnp.dot(kernel, direction_half, preferred_element_type=jnp.float32)
        sums = [jnp.sum(direction * direction, axis=0)]
        if norm_now is None:
            sums.append(jnp.sum(residual * residual, axis=0))
        row_half, landmark_sums = halving_sum(
            row_part, jnp.concatenate(sums), "landmark", landmark_bits, jnp.bfloat16
        )
        column_count = direction.shape[1]
        direction_square = landmark_sums[:column_count]
        if norm_now is None:
            norm_now = landmark_sums[column_count:]
        row_square = jnp.sum(jnp.square(row_half.astype(jnp.float32)), axis=0)
        column_part = jnp.dot(kernel.T, row_half, preferred_element_type=jnp.float32)
        column_total, row_square_total = halving_sum(
            column_part, row_square, "sample", sample_bits, jnp.float32, jnp.float32
        )
        image = column_total / n_rows + ridge * direction
        curvature = row_square_total / n_rows + ridge * direction_square
        step_size = norm_now / curvature
        weights = weights + step_size * direction
        residual = residual - step_size * image
        norm_next = butterfly_sum(jnp.sum(residual * residual, axis=0), "landmark", landmark_bits)
        direction = residual + norm_next / norm_now * direction
        norm_now = norm_next
    return (weights, residual)


def solution(mesh):
    return jax.shard_map(
        on_device,
        mesh=mesh,
        in_specs=(
            P("sample", "landmark"),
            P("sample"),
            P("landmark", None),
            P("landmark"),
            P("landmark"),
            P(),
            P("sample", None),
        ),
        out_specs=(P("landmark", None), P("landmark", None)),
        check_vma=False,
    )
```

```python
import math

import jax
import jax.numpy as jnp
from jax import lax
from jax.sharding import PartitionSpec as P

ITERS = 2
GROUPS = 2


ridge = 0.5


def level_values(level_ids, level_table):
    onehot = level_ids[:, None] == jnp.arange(level_table.shape[0], dtype=jnp.int32)[None, :]
    return jnp.sum(
        jnp.where(onehot, level_table[None, :], jnp.zeros_like(level_table)[None, :]), axis=1
    )


def raw_block(summary_rows, row_factor, anchors, anchor_factor):
    scores = jnp.dot(summary_rows, anchors.T, preferred_element_type=jnp.float32)
    return jnp.exp(scores * row_factor[:, None] * anchor_factor[None, :])


def partner_bits(size, order):
    bits = [b for b in order if b < size]
    assert sorted(bits) == [1 << i for i in range(size.bit_length() - 1)]
    return bits


def butterfly_sum(x, axis, bits):
    size = lax.axis_size(axis)
    for k in bits:
        perm = [(i, i ^ k) for i in range(size)]
        x = x + lax.ppermute(x, axis, perm)
    return x


def halving_sum(x, extra, axis, bits, gather_dtype, wire_dtype=jnp.bfloat16):
    size = lax.axis_size(axis)
    index = lax.axis_index(axis)
    for k in bits:
        perm = [(i, i ^ k) for i in range(size)]
        half = x.shape[0] // 2
        mine = (index // k) % 2
        keep = lax.dynamic_slice_in_dim(x, mine * half, half, axis=0)
        send = lax.dynamic_slice_in_dim(x, (1 - mine) * half, half, axis=0)
        got, got_extra = lax.ppermute((send.astype(wire_dtype), extra), axis, perm)
        x = keep + got.astype(jnp.float32)
        extra = extra + got_extra
    x = x.astype(gather_dtype)
    for k in reversed(bits):
        perm = [(i, i ^ k) for i in range(size)]
        part = x.shape[0]
        mine = (index // k) % 2
        got = lax.ppermute(x, axis, perm)
        whole = jnp.zeros((2 * part,) + x.shape[1:], x.dtype)
        whole = lax.dynamic_update_slice_in_dim(whole, x, mine * part, axis=0)
        x = lax.dynamic_update_slice_in_dim(whole, got, (1 - mine) * part, axis=0)
    return x, extra


def conjugate_gradients(kernel, targets, n_rows, sample_bits, landmark_bits):
    rhs_part = jnp.dot(kernel.T, targets, preferred_element_type=jnp.float32)
    rhs_total, _ = halving_sum(
        rhs_part, jnp.zeros((1,), jnp.float32), "sample", sample_bits, jnp.float32, jnp.float32
    )
    rhs = rhs_total / math.sqrt(n_rows)
    weights = jnp.zeros_like(rhs)
    residual = rhs
    direction = rhs
    norm_now = None
    for iteration in range(ITERS):
        direction_half = direction.astype(jnp.bfloat16)
        row_part = jnp.dot(kernel, direction_half, preferred_element_type=jnp.float32)
        sums = [jnp.sum(direction * direction, axis=0)]
        if norm_now is None:
            sums.append(jnp.sum(residual * residual, axis=0))
        row_half, landmark_sums = halving_sum(
            row_part, jnp.concatenate(sums), "landmark", landmark_bits, jnp.bfloat16
        )
        column_count = direction.shape[1]
        direction_square = landmark_sums[:column_count]
        if norm_now is None:
            norm_now = landmark_sums[column_count:]
        row_square = jnp.sum(jnp.square(row_half.astype(jnp.float32)), axis=0)
        column_part = jnp.dot(kernel.T, row_half, preferred_element_type=jnp.float32)
        column_total, row_square_total = halving_sum(
            column_part, row_square, "sample", sample_bits, jnp.float32, jnp.float32
        )
        image = column_total / n_rows + ridge * direction
        curvature = row_square_total / n_rows + ridge * direction_square
        step_size = norm_now / curvature
        weights = weights + step_size * direction
        residual = residual - step_size * image
        norm_next = butterfly_sum(jnp.sum(residual * residual, axis=0), "landmark", landmark_bits)
        direction = residual + norm_next / norm_now * direction
        norm_now = norm_next
    return weights, residual


def on_device(summaries, row_level, pool, pool_level, landmark_index, level_scale, targets):
    sample_bits = partner_bits(lax.axis_size("sample"), (2, 1, 4, 8, 16, 32, 64))
    landmark_bits = partner_bits(lax.axis_size("landmark"), (1, 2, 4, 8, 16, 32, 64))
    row_count = summaries.shape[0]
    n_rows = row_count * lax.axis_size("sample")
    gathered = lax.all_gather(summaries, "landmark", axis=1, tiled=True)
    feature_count = gathered.shape[1]
    anchors = jnp.take(pool, landmark_index, axis=0)
    anchor_level = jnp.take(pool_level, landmark_index, axis=0)
    row_factor = 1.0 / math.sqrt(feature_count) / level_values(row_level, level_scale)
    anchor_factor = 1.0 / level_values(anchor_level, level_scale)
    raw = raw_block(gathered, row_factor, anchors, anchor_factor)
    column_mean = butterfly_sum(jnp.sum(raw, axis=0), "sample", sample_bits) / n_rows
    kernel = (raw - column_mean[None, :]).astype(jnp.bfloat16)
    column_count = targets.shape[1]
    group_width = column_count // GROUPS
    results = [
        conjugate_gradients(
            kernel, targets[:, g * group_width:(g + 1) * group_width], n_rows, sample_bits, landmark_bits
        )
        for g in range(GROUPS)
    ]
    weights = jnp.concatenate([r[0] for r in results], axis=1)
    residual = jnp.concatenate([r[1] for r in results], axis=1)
    return (weights, residual)


def solution(mesh):
    return jax.shard_map(
        on_device,
        mesh=mesh,
        in_specs=(
            P("sample", "landmark"),
            P("sample"),
            P("landmark", None),
            P("landmark"),
            P("landmark"),
            P(),
            P("sample", None),
        ),
        out_specs=(P("landmark", None), P("landmark", None)),
        check_vma=False,
    )
```

```python
import math

import jax
import jax.numpy as jnp
from jax import lax
from jax.sharding import PartitionSpec as P

ITERS = 2
GROUPS = 2


ridge = 0.5


def level_values(level_ids, level_table):
    onehot = level_ids[:, None] == jnp.arange(level_table.shape[0], dtype=jnp.int32)[None, :]
    return jnp.sum(
        jnp.where(onehot, level_table[None, :], jnp.zeros_like(level_table)[None, :]), axis=1
    )


def raw_block(summary_rows, row_factor, anchors, anchor_factor):
    scores = jnp.dot(summary_rows, anchors.T, preferred_element_type=jnp.float32)
    return jnp.exp(scores * row_factor[:, None] * anchor_factor[None, :])


def partner_bits(size, order):
    bits = [b for b in order if b < size]
    assert sorted(bits) == [1 << i for i in range(size.bit_length() - 1)]
    return bits


def butterfly_sum(x, axis, bits):
    size = lax.axis_size(axis)
    for k in bits:
        perm = [(i, i ^ k) for i in range(size)]
        x = x + lax.ppermute(x, axis, perm)
    return x


def pack_rows(extra, columns, wire_dtype):
    rows = extra.reshape(-1, columns)
    if wire_dtype == jnp.float32:
        parts = [rows]
    else:
        parts = []
        rest = rows
        for _ in range(3):
            term = rest.astype(wire_dtype)
            parts.append(term)
            rest = rest - term.astype(jnp.float32)
    return jnp.concatenate(parts, axis=0).astype(wire_dtype)


def unpack_rows(packed, count, wire_dtype):
    terms = 1 if wire_dtype == jnp.float32 else 3
    packed = packed.astype(jnp.float32).reshape(terms, count, -1)
    total = packed[0]
    for t in range(1, terms):
        total = total + packed[t]
    return total.reshape(-1)


def halving_sum(x, extra, axis, bits, gather_dtype, wire_dtype=jnp.bfloat16):
    size = lax.axis_size(axis)
    index = lax.axis_index(axis)
    columns = x.shape[1]
    for k in bits:
        perm = [(i, i ^ k) for i in range(size)]
        half = x.shape[0] // 2
        mine = (index // k) % 2
        keep = lax.dynamic_slice_in_dim(x, mine * half, half, axis=0)
        send = lax.dynamic_slice_in_dim(x, (1 - mine) * half, half, axis=0).astype(wire_dtype)
        if extra is not None:
            send = jnp.concatenate([send, pack_rows(extra, columns, wire_dtype)], axis=0)
        got = lax.ppermute(send, axis, perm)
        x = keep + got[:half].astype(jnp.float32)
        if extra is not None:
            extra = extra + unpack_rows(got[half:], extra.shape[0] // columns, wire_dtype)
    x = x.astype(gather_dtype)
    for k in reversed(bits):
        perm = [(i, i ^ k) for i in range(size)]
        part = x.shape[0]
        mine = (index // k) % 2
        got = lax.ppermute(x, axis, perm)
        whole = jnp.zeros((2 * part,) + x.shape[1:], x.dtype)
        whole = lax.dynamic_update_slice_in_dim(whole, x, mine * part, axis=0)
        x = lax.dynamic_update_slice_in_dim(whole, got, (1 - mine) * part, axis=0)
    return x, extra


def conjugate_gradients(kernel, targets, n_rows, sample_bits, landmark_bits):
    rhs_part = jnp.dot(kernel.T, targets, preferred_element_type=jnp.float32)
    rhs_total, _ = halving_sum(
        rhs_part, None, "sample", sample_bits, jnp.float32, jnp.float32
    )
    rhs = rhs_total / math.sqrt(n_rows)
    weights = jnp.zeros_like(rhs)
    residual = rhs
    direction = rhs
    norm_now = None
    for iteration in range(ITERS):
        direction_half = direction.astype(jnp.bfloat16)
        row_part = jnp.dot(kernel, direction_half, preferred_element_type=jnp.float32)
        sums = [jnp.sum(direction * direction, axis=0)]
        if norm_now is None:
            sums.append(jnp.sum(residual * residual, axis=0))
        row_half, landmark_sums = halving_sum(
            row_part, jnp.concatenate(sums), "landmark", landmark_bits, jnp.bfloat16
        )
        column_count = direction.shape[1]
        direction_square = landmark_sums[:column_count]
        if norm_now is None:
            norm_now = landmark_sums[column_count:]
        row_square = jnp.sum(jnp.square(row_half.astype(jnp.float32)), axis=0)
        column_part = jnp.dot(kernel.T, row_half, preferred_element_type=jnp.float32)
        column_total, row_square_total = halving_sum(
            column_part, row_square, "sample", sample_bits, jnp.float32, jnp.float32
        )
        image = column_total / n_rows + ridge * direction
        curvature = row_square_total / n_rows + ridge * direction_square
        step_size = norm_now / curvature
        weights = weights + step_size * direction
        residual = residual - step_size * image
        norm_next = butterfly_sum(jnp.sum(residual * residual, axis=0), "landmark", landmark_bits)
        direction = residual + norm_next / norm_now * direction
        norm_now = norm_next
    return weights, residual


def on_device(summaries, row_level, pool, pool_level, landmark_index, level_scale, targets):
    sample_bits = partner_bits(lax.axis_size("sample"), (2, 1, 4, 8, 16, 32, 64))
    landmark_bits = partner_bits(lax.axis_size("landmark"), (1, 2, 4, 8, 16, 32, 64))
    row_count = summaries.shape[0]
    n_rows = row_count * lax.axis_size("sample")
    gathered = lax.all_gather(summaries, "landmark", axis=1, tiled=True)
    feature_count = gathered.shape[1]
    anchors = jnp.take(pool, landmark_index, axis=0)
    anchor_level = jnp.take(pool_level, landmark_index, axis=0)
    row_factor = 1.0 / math.sqrt(feature_count) / level_values(row_level, level_scale)
    anchor_factor = 1.0 / level_values(anchor_level, level_scale)
    raw = raw_block(gathered, row_factor, anchors, anchor_factor)
    column_mean = butterfly_sum(jnp.sum(raw, axis=0), "sample", sample_bits) / n_rows
    kernel = (raw - column_mean[None, :]).astype(jnp.bfloat16)
    column_count = targets.shape[1]
    group_width = column_count // GROUPS
    results = [
        conjugate_gradients(
            kernel, targets[:, g * group_width:(g + 1) * group_width], n_rows, sample_bits, landmark_bits
        )
        for g in range(GROUPS)
    ]
    weights = jnp.concatenate([r[0] for r in results], axis=1)
    residual = jnp.concatenate([r[1] for r in results], axis=1)
    return (weights, residual)


def solution(mesh):
    return jax.shard_map(
        on_device,
        mesh=mesh,
        in_specs=(
            P("sample", "landmark"),
            P("sample"),
            P("landmark", None),
            P("landmark"),
            P("landmark"),
            P(),
            P("sample", None),
        ),
        out_specs=(P("landmark", None), P("landmark", None)),
        check_vma=False,
    )
```

```python
import math

import jax
import jax.numpy as jnp
from jax import lax
from jax.sharding import PartitionSpec as P

ITERS = 2
GROUPS = 2


ridge = 0.5


def level_values(level_ids, level_table):
    onehot = level_ids[:, None] == jnp.arange(level_table.shape[0], dtype=jnp.int32)[None, :]
    return jnp.sum(
        jnp.where(onehot, level_table[None, :], jnp.zeros_like(level_table)[None, :]), axis=1
    )


def raw_block(summary_rows, row_factor, anchors, anchor_factor):
    scores = jnp.dot(summary_rows, anchors.T, preferred_element_type=jnp.float32)
    return jnp.exp(scores * row_factor[:, None] * anchor_factor[None, :])


def partner_bits(size, order):
    bits = [b for b in order if b < size]
    assert sorted(bits) == [1 << i for i in range(size.bit_length() - 1)]
    return bits


def butterfly_sum(x, axis, bits):
    size = lax.axis_size(axis)
    for k in bits:
        perm = [(i, i ^ k) for i in range(size)]
        x = x + lax.ppermute(x, axis, perm)
    return x


def pack_rows(extra, columns, wire_dtype):
    rows = extra.reshape(-1, columns)
    if wire_dtype == jnp.float32:
        parts = [rows]
    else:
        parts = []
        rest = rows
        for _ in range(3):
            term = lax.reduce_precision(rest, exponent_bits=8, mantissa_bits=7)
            parts.append(term)
            rest = rest - term
    return jnp.concatenate(parts, axis=0).astype(wire_dtype)


def unpack_rows(packed, count, wire_dtype):
    terms = 1 if wire_dtype == jnp.float32 else 3
    packed = packed.astype(jnp.float32).reshape(terms, count, -1)
    total = packed[0]
    for t in range(1, terms):
        total = total + packed[t]
    return total.reshape(-1)


def halving_sum(x, extra, axis, bits, gather_dtype, wire_dtype=jnp.bfloat16):
    size = lax.axis_size(axis)
    index = lax.axis_index(axis)
    columns = x.shape[1]
    for k in bits:
        perm = [(i, i ^ k) for i in range(size)]
        half = x.shape[0] // 2
        mine = (index // k) % 2
        keep = lax.dynamic_slice_in_dim(x, mine * half, half, axis=0)
        send = lax.dynamic_slice_in_dim(x, (1 - mine) * half, half, axis=0).astype(wire_dtype)
        if extra is not None:
            send = jnp.concatenate([send, pack_rows(extra, columns, wire_dtype)], axis=0)
        got = lax.ppermute(send, axis, perm)
        x = keep + got[:half].astype(jnp.float32)
        if extra is not None:
            extra = extra + unpack_rows(got[half:], extra.shape[0] // columns, wire_dtype)
    x = x.astype(gather_dtype)
    for k in reversed(bits):
        perm = [(i, i ^ k) for i in range(size)]
        part = x.shape[0]
        mine = (index // k) % 2
        got = lax.ppermute(x, axis, perm)
        whole = jnp.zeros((2 * part,) + x.shape[1:], x.dtype)
        whole = lax.dynamic_update_slice_in_dim(whole, x, mine * part, axis=0)
        x = lax.dynamic_update_slice_in_dim(whole, got, (1 - mine) * part, axis=0)
    return x, extra


def conjugate_gradients(kernel, targets, n_rows, sample_bits, landmark_bits):
    rhs_part = jnp.dot(kernel.T, targets, preferred_element_type=jnp.float32)
    rhs_total, _ = halving_sum(
        rhs_part, None, "sample", sample_bits, jnp.float32, jnp.float32
    )
    rhs = rhs_total / math.sqrt(n_rows)
    weights = jnp.zeros_like(rhs)
    residual = rhs
    direction = rhs
    norm_now = None
    for iteration in range(ITERS):
        direction_half = direction.astype(jnp.bfloat16)
        row_part = jnp.dot(kernel, direction_half, preferred_element_type=jnp.float32)
        sums = [jnp.sum(direction * direction, axis=0)]
        if norm_now is None:
            sums.append(jnp.sum(residual * residual, axis=0))
        row_half, landmark_sums = halving_sum(
            row_part, jnp.concatenate(sums), "landmark", landmark_bits, jnp.bfloat16
        )
        column_count = direction.shape[1]
        direction_square = landmark_sums[:column_count]
        if norm_now is None:
            norm_now = landmark_sums[column_count:]
        row_square = jnp.sum(jnp.square(row_half.astype(jnp.float32)), axis=0)
        column_part = jnp.dot(kernel.T, row_half, preferred_element_type=jnp.float32)
        column_total, row_square_total = halving_sum(
            column_part, row_square, "sample", sample_bits, jnp.float32, jnp.float32
        )
        image = column_total / n_rows + ridge * direction
        curvature = row_square_total / n_rows + ridge * direction_square
        step_size = norm_now / curvature
        weights = weights + step_size * direction
        residual = residual - step_size * image
        norm_next = butterfly_sum(jnp.sum(residual * residual, axis=0), "landmark", landmark_bits)
        direction = residual + norm_next / norm_now * direction
        norm_now = norm_next
    return weights, residual


def on_device(summaries, row_level, pool, pool_level, landmark_index, level_scale, targets):
    sample_bits = partner_bits(lax.axis_size("sample"), (2, 1, 4, 8, 16, 32, 64))
    landmark_bits = partner_bits(lax.axis_size("landmark"), (1, 2, 4, 8, 16, 32, 64))
    row_count = summaries.shape[0]
    n_rows = row_count * lax.axis_size("sample")
    gathered = lax.all_gather(summaries, "landmark", axis=1, tiled=True)
    feature_count = gathered.shape[1]
    anchors = jnp.take(pool, landmark_index, axis=0)
    anchor_level = jnp.take(pool_level, landmark_index, axis=0)
    row_factor = 1.0 / math.sqrt(feature_count) / level_values(row_level, level_scale)
    anchor_factor = 1.0 / level_values(anchor_level, level_scale)
    raw = raw_block(gathered, row_factor, anchors, anchor_factor)
    column_mean = butterfly_sum(jnp.sum(raw, axis=0), "sample", sample_bits) / n_rows
    kernel = (raw - column_mean[None, :]).astype(jnp.bfloat16)
    column_count = targets.shape[1]
    group_width = column_count // GROUPS
    results = [
        conjugate_gradients(
            kernel, targets[:, g * group_width:(g + 1) * group_width], n_rows, sample_bits, landmark_bits
        )
        for g in range(GROUPS)
    ]
    weights = jnp.concatenate([r[0] for r in results], axis=1)
    residual = jnp.concatenate([r[1] for r in results], axis=1)
    return (weights, residual)


def solution(mesh):
    return jax.shard_map(
        on_device,
        mesh=mesh,
        in_specs=(
            P("sample", "landmark"),
            P("sample"),
            P("landmark", None),
            P("landmark"),
            P("landmark"),
            P(),
            P("sample", None),
        ),
        out_specs=(P("landmark", None), P("landmark", None)),
        check_vma=False,
    )
```

```python
import math

import jax
import jax.numpy as jnp
from jax import lax
from jax.sharding import PartitionSpec as P

ITERS = 2
GROUPS = 1


def REDUCE(x, extra, axis, bits, gather_dtype, wire_dtype=jnp.bfloat16):
    return exchange_sum(x, extra, axis, gather_dtype, wire_dtype)


ridge = 0.5


def level_values(level_ids, level_table):
    onehot = level_ids[:, None] == jnp.arange(level_table.shape[0], dtype=jnp.int32)[None, :]
    return jnp.sum(
        jnp.where(onehot, level_table[None, :], jnp.zeros_like(level_table)[None, :]), axis=1
    )


def raw_block(summary_rows, row_factor, anchors, anchor_factor):
    scores = jnp.dot(summary_rows, anchors.T, preferred_element_type=jnp.float32)
    return jnp.exp(scores * row_factor[:, None] * anchor_factor[None, :])


def partner_bits(size, order):
    bits = [b for b in order if b < size]
    assert sorted(bits) == [1 << i for i in range(size.bit_length() - 1)]
    return bits


def butterfly_sum(x, axis, bits):
    size = lax.axis_size(axis)
    for k in bits:
        perm = [(i, i ^ k) for i in range(size)]
        x = x + lax.ppermute(x, axis, perm)
    return x


def pack_rows(extra, columns, wire_dtype):
    rows = extra.reshape(-1, columns)
    if wire_dtype == jnp.float32:
        parts = [rows]
    else:
        parts = []
        rest = rows
        for _ in range(3):
            term = lax.reduce_precision(rest, exponent_bits=8, mantissa_bits=7)
            parts.append(term)
            rest = rest - term
    return jnp.concatenate(parts, axis=0).astype(wire_dtype)


def unpack_rows(packed, count, wire_dtype):
    terms = 1 if wire_dtype == jnp.float32 else 3
    packed = packed.astype(jnp.float32).reshape(terms, count, -1)
    total = packed[0]
    for t in range(1, terms):
        total = total + packed[t]
    return total.reshape(-1)


def halving_sum(x, extra, axis, bits, gather_dtype, wire_dtype=jnp.bfloat16):
    size = lax.axis_size(axis)
    index = lax.axis_index(axis)
    columns = x.shape[1]
    for k in bits:
        perm = [(i, i ^ k) for i in range(size)]
        half = x.shape[0] // 2
        mine = (index // k) % 2
        keep = lax.dynamic_slice_in_dim(x, mine * half, half, axis=0)
        send = lax.dynamic_slice_in_dim(x, (1 - mine) * half, half, axis=0).astype(wire_dtype)
        if extra is not None:
            send = jnp.concatenate([send, pack_rows(extra, columns, wire_dtype)], axis=0)
        got = lax.ppermute(send, axis, perm)
        x = keep + got[:half].astype(jnp.float32)
        if extra is not None:
            extra = extra + unpack_rows(got[half:], extra.shape[0] // columns, wire_dtype)
    x = x.astype(gather_dtype)
    for k in reversed(bits):
        perm = [(i, i ^ k) for i in range(size)]
        part = x.shape[0]
        mine = (index // k) % 2
        got = lax.ppermute(x, axis, perm)
        whole = jnp.zeros((2 * part,) + x.shape[1:], x.dtype)
        whole = lax.dynamic_update_slice_in_dim(whole, x, mine * part, axis=0)
        x = lax.dynamic_update_slice_in_dim(whole, got, (1 - mine) * part, axis=0)
    return x, extra


def exchange_sum(x, extra, axis, gather_dtype, wire_dtype=jnp.bfloat16):
    size = lax.axis_size(axis)
    rows, columns = x.shape
    chunks = x.reshape(size, rows // size, columns).astype(wire_dtype)
    if extra is not None:
        packed = pack_rows(extra, columns, wire_dtype)
        chunks = jnp.concatenate(
            [chunks, jnp.broadcast_to(packed[None], (size,) + packed.shape)], axis=1
        )
    got = lax.all_to_all(chunks, axis, 0, 0, tiled=False)
    total = jnp.sum(got.astype(jnp.float32), axis=0)
    part = total[: rows // size].astype(gather_dtype)
    if extra is not None:
        extra = unpack_rows(total[rows // size:], extra.shape[0] // columns, wire_dtype)
    whole = lax.all_to_all(
        jnp.broadcast_to(part[None], (size,) + part.shape), axis, 0, 0, tiled=False
    )
    return whole.reshape(rows, columns), extra


def conjugate_gradients(kernel, targets, n_rows, sample_bits, landmark_bits):
    rhs_part = jnp.dot(kernel.T, targets, preferred_element_type=jnp.float32)
    rhs_total, _ = REDUCE(rhs_part, None, "sample", sample_bits, jnp.float32, jnp.float32)
    rhs = rhs_total / math.sqrt(n_rows)
    weights = jnp.zeros_like(rhs)
    residual = rhs
    direction = rhs
    norm_now = None
    for iteration in range(ITERS):
        direction_half = direction.astype(jnp.bfloat16)
        row_part = jnp.dot(kernel, direction_half, preferred_element_type=jnp.float32)
        sums = [jnp.sum(direction * direction, axis=0)]
        if norm_now is None:
            sums.append(jnp.sum(residual * residual, axis=0))
        row_half, landmark_sums = REDUCE(
            row_part, jnp.concatenate(sums), "landmark", landmark_bits, jnp.bfloat16
        )
        column_count = direction.shape[1]
        direction_square = landmark_sums[:column_count]
        if norm_now is None:
            norm_now = landmark_sums[column_count:]
        row_square = jnp.sum(jnp.square(row_half.astype(jnp.float32)), axis=0)
        column_part = jnp.dot(kernel.T, row_half, preferred_element_type=jnp.float32)
        column_total, row_square_total = REDUCE(
            column_part, row_square, "sample", sample_bits, jnp.float32, jnp.float32
        )
        image = column_total / n_rows + ridge * direction
        curvature = row_square_total / n_rows + ridge * direction_square
        step_size = norm_now / curvature
        weights = weights + step_size * direction
        residual = residual - step_size * image
        norm_next = butterfly_sum(jnp.sum(residual * residual, axis=0), "landmark", landmark_bits)
        direction = residual + norm_next / norm_now * direction
        norm_now = norm_next
    return weights, residual


def on_device(summaries, row_level, pool, pool_level, landmark_index, level_scale, targets):
    sample_bits = partner_bits(lax.axis_size("sample"), (2, 1, 4, 8, 16, 32, 64))
    landmark_bits = partner_bits(lax.axis_size("landmark"), (1, 2, 4, 8, 16, 32, 64))
    row_count = summaries.shape[0]
    n_rows = row_count * lax.axis_size("sample")
    gathered = lax.all_gather(summaries, "landmark", axis=1, tiled=True)
    feature_count = gathered.shape[1]
    anchors = jnp.take(pool, landmark_index, axis=0)
    anchor_level = jnp.take(pool_level, landmark_index, axis=0)
    row_factor = 1.0 / math.sqrt(feature_count) / level_values(row_level, level_scale)
    anchor_factor = 1.0 / level_values(anchor_level, level_scale)
    raw = raw_block(gathered, row_factor, anchors, anchor_factor)
    column_mean = butterfly_sum(jnp.sum(raw, axis=0), "sample", sample_bits) / n_rows
    kernel = (raw - column_mean[None, :]).astype(jnp.bfloat16)
    column_count = targets.shape[1]
    group_width = column_count // GROUPS
    results = [
        conjugate_gradients(
            kernel, targets[:, g * group_width:(g + 1) * group_width], n_rows, sample_bits, landmark_bits
        )
        for g in range(GROUPS)
    ]
    weights = jnp.concatenate([r[0] for r in results], axis=1)
    residual = jnp.concatenate([r[1] for r in results], axis=1)
    return (weights, residual)


def solution(mesh):
    return jax.shard_map(
        on_device,
        mesh=mesh,
        in_specs=(
            P("sample", "landmark"),
            P("sample"),
            P("landmark", None),
            P("landmark"),
            P("landmark"),
            P(),
            P("sample", None),
        ),
        out_specs=(P("landmark", None), P("landmark", None)),
        check_vma=False,
    )
```

```python
import math

import jax
import jax.numpy as jnp
from jax import lax
from jax.sharding import PartitionSpec as P

ITERS = 2
GROUPS = 2


def REDUCE(x, extra, axis, bits, gather_dtype, wire_dtype=jnp.bfloat16):
    return exchange_sum(x, extra, axis, gather_dtype, wire_dtype)


ridge = 0.5


def level_values(level_ids, level_table):
    onehot = level_ids[:, None] == jnp.arange(level_table.shape[0], dtype=jnp.int32)[None, :]
    return jnp.sum(
        jnp.where(onehot, level_table[None, :], jnp.zeros_like(level_table)[None, :]), axis=1
    )


def raw_block(summary_rows, row_factor, anchors, anchor_factor):
    scores = jnp.dot(summary_rows, anchors.T, preferred_element_type=jnp.float32)
    return jnp.exp(scores * row_factor[:, None] * anchor_factor[None, :])


def partner_bits(size, order):
    bits = [b for b in order if b < size]
    assert sorted(bits) == [1 << i for i in range(size.bit_length() - 1)]
    return bits


def butterfly_sum(x, axis, bits):
    size = lax.axis_size(axis)
    for k in bits:
        perm = [(i, i ^ k) for i in range(size)]
        x = x + lax.ppermute(x, axis, perm)
    return x


def pack_rows(extra, columns, wire_dtype):
    rows = extra.reshape(-1, columns)
    if wire_dtype == jnp.float32:
        parts = [rows]
    else:
        parts = []
        rest = rows
        for _ in range(3):
            term = lax.reduce_precision(rest, exponent_bits=8, mantissa_bits=7)
            parts.append(term)
            rest = rest - term
    return jnp.concatenate(parts, axis=0).astype(wire_dtype)


def unpack_rows(packed, count, wire_dtype):
    terms = 1 if wire_dtype == jnp.float32 else 3
    packed = packed.astype(jnp.float32).reshape(terms, count, -1)
    total = packed[0]
    for t in range(1, terms):
        total = total + packed[t]
    return total.reshape(-1)


def halving_sum(x, extra, axis, bits, gather_dtype, wire_dtype=jnp.bfloat16):
    size = lax.axis_size(axis)
    index = lax.axis_index(axis)
    columns = x.shape[1]
    for k in bits:
        perm = [(i, i ^ k) for i in range(size)]
        half = x.shape[0] // 2
        mine = (index // k) % 2
        keep = lax.dynamic_slice_in_dim(x, mine * half, half, axis=0)
        send = lax.dynamic_slice_in_dim(x, (1 - mine) * half, half, axis=0).astype(wire_dtype)
        if extra is not None:
            send = jnp.concatenate([send, pack_rows(extra, columns, wire_dtype)], axis=0)
        got = lax.ppermute(send, axis, perm)
        x = keep + got[:half].astype(jnp.float32)
        if extra is not None:
            extra = extra + unpack_rows(got[half:], extra.shape[0] // columns, wire_dtype)
    x = x.astype(gather_dtype)
    for k in reversed(bits):
        perm = [(i, i ^ k) for i in range(size)]
        part = x.shape[0]
        mine = (index // k) % 2
        got = lax.ppermute(x, axis, perm)
        whole = jnp.zeros((2 * part,) + x.shape[1:], x.dtype)
        whole = lax.dynamic_update_slice_in_dim(whole, x, mine * part, axis=0)
        x = lax.dynamic_update_slice_in_dim(whole, got, (1 - mine) * part, axis=0)
    return x, extra


def exchange_sum(x, extra, axis, gather_dtype, wire_dtype=jnp.bfloat16):
    size = lax.axis_size(axis)
    rows, columns = x.shape
    chunks = x.reshape(size, rows // size, columns).astype(wire_dtype)
    if extra is not None:
        packed = pack_rows(extra, columns, wire_dtype)
        chunks = jnp.concatenate(
            [chunks, jnp.broadcast_to(packed[None], (size,) + packed.shape)], axis=1
        )
    got = lax.all_to_all(chunks, axis, 0, 0, tiled=False)
    total = jnp.sum(got.astype(jnp.float32), axis=0)
    part = total[: rows // size].astype(gather_dtype)
    if extra is not None:
        extra = unpack_rows(total[rows // size:], extra.shape[0] // columns, wire_dtype)
    whole = lax.all_to_all(
        jnp.broadcast_to(part[None], (size,) + part.shape), axis, 0, 0, tiled=False
    )
    return whole.reshape(rows, columns), extra


def conjugate_gradients(kernel, targets, n_rows, sample_bits, landmark_bits):
    rhs_part = jnp.dot(kernel.T, targets, preferred_element_type=jnp.float32)
    rhs_total, _ = REDUCE(rhs_part, None, "sample", sample_bits, jnp.float32, jnp.float32)
    rhs = rhs_total / math.sqrt(n_rows)
    weights = jnp.zeros_like(rhs)
    residual = rhs
    direction = rhs
    norm_now = None
    for iteration in range(ITERS):
        direction_half = direction.astype(jnp.bfloat16)
        row_part = jnp.dot(kernel, direction_half, preferred_element_type=jnp.float32)
        sums = [jnp.sum(direction * direction, axis=0)]
        if norm_now is None:
            sums.append(jnp.sum(residual * residual, axis=0))
        row_half, landmark_sums = REDUCE(
            row_part, jnp.concatenate(sums), "landmark", landmark_bits, jnp.bfloat16
        )
        column_count = direction.shape[1]
        direction_square = landmark_sums[:column_count]
        if norm_now is None:
            norm_now = landmark_sums[column_count:]
        row_square = jnp.sum(jnp.square(row_half.astype(jnp.float32)), axis=0)
        column_part = jnp.dot(kernel.T, row_half, preferred_element_type=jnp.float32)
        column_total, row_square_total = REDUCE(
            column_part, row_square, "sample", sample_bits, jnp.float32, jnp.float32
        )
        image = column_total / n_rows + ridge * direction
        curvature = row_square_total / n_rows + ridge * direction_square
        step_size = norm_now / curvature
        weights = weights + step_size * direction
        residual = residual - step_size * image
        norm_next = butterfly_sum(jnp.sum(residual * residual, axis=0), "landmark", landmark_bits)
        direction = residual + norm_next / norm_now * direction
        norm_now = norm_next
    return weights, residual


def on_device(summaries, row_level, pool, pool_level, landmark_index, level_scale, targets):
    sample_bits = partner_bits(lax.axis_size("sample"), (2, 1, 4, 8, 16, 32, 64))
    landmark_bits = partner_bits(lax.axis_size("landmark"), (1, 2, 4, 8, 16, 32, 64))
    row_count = summaries.shape[0]
    n_rows = row_count * lax.axis_size("sample")
    gathered = lax.all_gather(summaries, "landmark", axis=1, tiled=True)
    feature_count = gathered.shape[1]
    anchors = jnp.take(pool, landmark_index, axis=0)
    anchor_level = jnp.take(pool_level, landmark_index, axis=0)
    row_factor = 1.0 / math.sqrt(feature_count) / level_values(row_level, level_scale)
    anchor_factor = 1.0 / level_values(anchor_level, level_scale)
    raw = raw_block(gathered, row_factor, anchors, anchor_factor)
    column_mean = butterfly_sum(jnp.sum(raw, axis=0), "sample", sample_bits) / n_rows
    kernel = (raw - column_mean[None, :]).astype(jnp.bfloat16)
    column_count = targets.shape[1]
    group_width = column_count // GROUPS
    results = [
        conjugate_gradients(
            kernel, targets[:, g * group_width:(g + 1) * group_width], n_rows, sample_bits, landmark_bits
        )
        for g in range(GROUPS)
    ]
    weights = jnp.concatenate([r[0] for r in results], axis=1)
    residual = jnp.concatenate([r[1] for r in results], axis=1)
    return (weights, residual)


def solution(mesh):
    return jax.shard_map(
        on_device,
        mesh=mesh,
        in_specs=(
            P("sample", "landmark"),
            P("sample"),
            P("landmark", None),
            P("landmark"),
            P("landmark"),
            P(),
            P("sample", None),
        ),
        out_specs=(P("landmark", None), P("landmark", None)),
        check_vma=False,
    )
```

```python
import math

import jax
import jax.numpy as jnp
from jax import lax
from jax.sharding import PartitionSpec as P

ITERS = 2
GROUPS = 1


def REDUCE(x, extra, axis, bits, gather_dtype, wire_dtype=jnp.bfloat16):
    return exchange_sum(x, extra, axis, gather_dtype, wire_dtype)


ridge = 0.5


def level_values(level_ids, level_table):
    onehot = level_ids[:, None] == jnp.arange(level_table.shape[0], dtype=jnp.int32)[None, :]
    return jnp.sum(
        jnp.where(onehot, level_table[None, :], jnp.zeros_like(level_table)[None, :]), axis=1
    )


def raw_block(summary_rows, row_factor, anchors, anchor_factor):
    scores = jnp.dot(summary_rows, anchors.T, preferred_element_type=jnp.float32)
    return jnp.exp(scores * row_factor[:, None] * anchor_factor[None, :])


def partner_bits(size, order):
    bits = [b for b in order if b < size]
    assert sorted(bits) == [1 << i for i in range(size.bit_length() - 1)]
    return bits


def butterfly_sum(x, axis, bits):
    size = lax.axis_size(axis)
    for k in bits:
        perm = [(i, i ^ k) for i in range(size)]
        x = x + lax.ppermute(x, axis, perm)
    return x


def pack_rows(extra, columns, wire_dtype):
    rows = extra.reshape(-1, columns)
    if wire_dtype == jnp.float32:
        parts = [rows]
    else:
        parts = []
        rest = rows
        for _ in range(3):
            term = lax.reduce_precision(rest, exponent_bits=8, mantissa_bits=7)
            parts.append(term)
            rest = rest - term
    return jnp.concatenate(parts, axis=0).astype(wire_dtype)


def unpack_rows(packed, count, wire_dtype):
    terms = 1 if wire_dtype == jnp.float32 else 3
    packed = packed.astype(jnp.float32).reshape(terms, count, -1)
    total = packed[0]
    for t in range(1, terms):
        total = total + packed[t]
    return total.reshape(-1)


def halving_sum(x, extra, axis, bits, gather_dtype, wire_dtype=jnp.bfloat16):
    size = lax.axis_size(axis)
    index = lax.axis_index(axis)
    columns = x.shape[1]
    for k in bits:
        perm = [(i, i ^ k) for i in range(size)]
        half = x.shape[0] // 2
        mine = (index // k) % 2
        keep = lax.dynamic_slice_in_dim(x, mine * half, half, axis=0)
        send = lax.dynamic_slice_in_dim(x, (1 - mine) * half, half, axis=0).astype(wire_dtype)
        if extra is not None:
            send = jnp.concatenate([send, pack_rows(extra, columns, wire_dtype)], axis=0)
        got = lax.ppermute(send, axis, perm)
        x = keep + got[:half].astype(jnp.float32)
        if extra is not None:
            extra = extra + unpack_rows(got[half:], extra.shape[0] // columns, wire_dtype)
    x = x.astype(gather_dtype)
    for k in reversed(bits):
        perm = [(i, i ^ k) for i in range(size)]
        part = x.shape[0]
        mine = (index // k) % 2
        got = lax.ppermute(x, axis, perm)
        whole = jnp.zeros((2 * part,) + x.shape[1:], x.dtype)
        whole = lax.dynamic_update_slice_in_dim(whole, x, mine * part, axis=0)
        x = lax.dynamic_update_slice_in_dim(whole, got, (1 - mine) * part, axis=0)
    return x, extra


def exchange_scatter(x, extra, axis, wire_dtype):
    size = lax.axis_size(axis)
    rows, columns = x.shape
    chunks = x.reshape(size, rows // size, columns).astype(wire_dtype)
    if extra is not None:
        packed = pack_rows(extra, columns, wire_dtype)
        chunks = jnp.concatenate(
            [chunks, jnp.broadcast_to(packed[None], (size,) + packed.shape)], axis=1
        )
    got = lax.all_to_all(chunks, axis, 0, 0, tiled=False)
    total = jnp.sum(got.astype(jnp.float32), axis=0)
    part = total[: rows // size]
    if extra is not None:
        extra = unpack_rows(total[rows // size:], extra.shape[0] // columns, wire_dtype)
    return part, extra


def exchange_gather(part, axis):
    size = lax.axis_size(axis)
    whole = lax.all_to_all(
        jnp.broadcast_to(part[None], (size,) + part.shape), axis, 0, 0, tiled=False
    )
    return whole.reshape((size * part.shape[0],) + part.shape[1:])


def exchange_sum(x, extra, axis, gather_dtype, wire_dtype=jnp.bfloat16):
    part, extra = exchange_scatter(x, extra, axis, wire_dtype)
    return exchange_gather(part.astype(gather_dtype), axis), extra


def conjugate_gradients(kernel, targets, n_rows, sample_bits, landmark_bits):
    rhs_part = jnp.dot(kernel.T, targets, preferred_element_type=jnp.float32)
    rhs_total, _ = exchange_sum(rhs_part, None, "sample", jnp.float32, jnp.float32)
    rhs = rhs_total / math.sqrt(n_rows)
    column_count = rhs.shape[1]
    weights = jnp.zeros_like(rhs)
    residual = rhs
    direction = rhs
    for iteration in range(ITERS):
        if iteration == 0:
            row_part = jnp.dot(kernel, direction.astype(jnp.bfloat16), preferred_element_type=jnp.float32)
            sums = jnp.concatenate(
                [jnp.sum(direction * direction, axis=0), jnp.sum(residual * residual, axis=0)]
            )
            row_chunk, landmark_sums = exchange_scatter(row_part, sums, "landmark", jnp.bfloat16)
            direction_square = landmark_sums[:column_count]
            norm_now = landmark_sums[column_count:]
        else:
            row_part = jnp.dot(kernel, residual.astype(jnp.bfloat16), preferred_element_type=jnp.float32)
            sums = jnp.concatenate(
                [jnp.sum(residual * residual, axis=0), jnp.sum(residual * direction, axis=0)]
            )
            residual_chunk, landmark_sums = exchange_scatter(row_part, sums, "landmark", jnp.bfloat16)
            norm_next = landmark_sums[:column_count]
            cross = landmark_sums[column_count:]
            beta = norm_next / norm_now
            row_chunk = residual_chunk + beta * row_chunk
            direction = residual + beta * direction
            direction_square = norm_next + 2.0 * beta * cross + beta * beta * direction_square
            norm_now = norm_next
        row_half = exchange_gather(row_chunk.astype(jnp.bfloat16), "landmark")
        row_square = jnp.sum(jnp.square(row_half.astype(jnp.float32)), axis=0)
        column_part = jnp.dot(kernel.T, row_half, preferred_element_type=jnp.float32)
        column_total, row_square_total = exchange_sum(
            column_part, row_square, "sample", jnp.float32, jnp.float32
        )
        image = column_total / n_rows + ridge * direction
        curvature = row_square_total / n_rows + ridge * direction_square
        step_size = norm_now / curvature
        weights = weights + step_size * direction
        residual = residual - step_size * image
    return weights, residual


def on_device(summaries, row_level, pool, pool_level, landmark_index, level_scale, targets):
    sample_bits = partner_bits(lax.axis_size("sample"), (2, 1, 4, 8, 16, 32, 64))
    landmark_bits = partner_bits(lax.axis_size("landmark"), (1, 2, 4, 8, 16, 32, 64))
    row_count = summaries.shape[0]
    n_rows = row_count * lax.axis_size("sample")
    gathered = lax.all_gather(summaries, "landmark", axis=1, tiled=True)
    feature_count = gathered.shape[1]
    anchors = jnp.take(pool, landmark_index, axis=0)
    anchor_level = jnp.take(pool_level, landmark_index, axis=0)
    row_factor = 1.0 / math.sqrt(feature_count) / level_values(row_level, level_scale)
    anchor_factor = 1.0 / level_values(anchor_level, level_scale)
    raw = raw_block(gathered, row_factor, anchors, anchor_factor)
    column_mean = butterfly_sum(jnp.sum(raw, axis=0), "sample", sample_bits) / n_rows
    kernel = (raw - column_mean[None, :]).astype(jnp.bfloat16)
    column_count = targets.shape[1]
    group_width = column_count // GROUPS
    results = [
        conjugate_gradients(
            kernel, targets[:, g * group_width:(g + 1) * group_width], n_rows, sample_bits, landmark_bits
        )
        for g in range(GROUPS)
    ]
    weights = jnp.concatenate([r[0] for r in results], axis=1)
    residual = jnp.concatenate([r[1] for r in results], axis=1)
    return (weights, residual)


def solution(mesh):
    return jax.shard_map(
        on_device,
        mesh=mesh,
        in_specs=(
            P("sample", "landmark"),
            P("sample"),
            P("landmark", None),
            P("landmark"),
            P("landmark"),
            P(),
            P("sample", None),
        ),
        out_specs=(P("landmark", None), P("landmark", None)),
        check_vma=False,
    )
```

```python
import math

import jax
import jax.numpy as jnp
from jax import lax
from jax.sharding import PartitionSpec as P

ITERS = 2
GROUPS = 1


def REDUCE(x, extra, axis, bits, gather_dtype, wire_dtype=jnp.bfloat16):
    return exchange_sum(x, extra, axis, gather_dtype, wire_dtype)


ridge = 0.5


def level_values(level_ids, level_table):
    onehot = level_ids[:, None] == jnp.arange(level_table.shape[0], dtype=jnp.int32)[None, :]
    return jnp.sum(
        jnp.where(onehot, level_table[None, :], jnp.zeros_like(level_table)[None, :]), axis=1
    )


def raw_block(summary_rows, row_factor, anchors, anchor_factor):
    scores = jnp.dot(summary_rows, anchors.T, preferred_element_type=jnp.float32)
    return jnp.exp(scores * row_factor[:, None] * anchor_factor[None, :])


def partner_bits(size, order):
    bits = [b for b in order if b < size]
    assert sorted(bits) == [1 << i for i in range(size.bit_length() - 1)]
    return bits


def butterfly_sum(x, axis, bits):
    size = lax.axis_size(axis)
    for k in bits:
        perm = [(i, i ^ k) for i in range(size)]
        x = x + lax.ppermute(x, axis, perm)
    return x


def pack_rows(extra, columns, wire_dtype):
    rows = extra.reshape(-1, columns)
    if wire_dtype == jnp.float32:
        parts = [rows]
    else:
        parts = []
        rest = rows
        for _ in range(3):
            term = lax.reduce_precision(rest, exponent_bits=8, mantissa_bits=7)
            parts.append(term)
            rest = rest - term
    return jnp.concatenate(parts, axis=0).astype(wire_dtype)


def unpack_rows(packed, count, wire_dtype):
    terms = 1 if wire_dtype == jnp.float32 else 3
    packed = packed.astype(jnp.float32).reshape(terms, count, -1)
    total = packed[0]
    for t in range(1, terms):
        total = total + packed[t]
    return total.reshape(-1)


def halving_sum(x, extra, axis, bits, gather_dtype, wire_dtype=jnp.bfloat16):
    size = lax.axis_size(axis)
    index = lax.axis_index(axis)
    columns = x.shape[1]
    for k in bits:
        perm = [(i, i ^ k) for i in range(size)]
        half = x.shape[0] // 2
        mine = (index // k) % 2
        keep = lax.dynamic_slice_in_dim(x, mine * half, half, axis=0)
        send = lax.dynamic_slice_in_dim(x, (1 - mine) * half, half, axis=0).astype(wire_dtype)
        if extra is not None:
            send = jnp.concatenate([send, pack_rows(extra, columns, wire_dtype)], axis=0)
        got = lax.ppermute(send, axis, perm)
        x = keep + got[:half].astype(jnp.float32)
        if extra is not None:
            extra = extra + unpack_rows(got[half:], extra.shape[0] // columns, wire_dtype)
    x = x.astype(gather_dtype)
    for k in reversed(bits):
        perm = [(i, i ^ k) for i in range(size)]
        part = x.shape[0]
        mine = (index // k) % 2
        got = lax.ppermute(x, axis, perm)
        whole = jnp.zeros((2 * part,) + x.shape[1:], x.dtype)
        whole = lax.dynamic_update_slice_in_dim(whole, x, mine * part, axis=0)
        x = lax.dynamic_update_slice_in_dim(whole, got, (1 - mine) * part, axis=0)
    return x, extra


def exchange_scatter(x, extra, axis, wire_dtype):
    size = lax.axis_size(axis)
    rows, columns = x.shape
    chunks = x.reshape(size, rows // size, columns).astype(wire_dtype)
    if extra is not None:
        packed = pack_rows(extra, columns, wire_dtype)
        chunks = jnp.concatenate(
            [chunks, jnp.broadcast_to(packed[None], (size,) + packed.shape)], axis=1
        )
    got = lax.all_to_all(chunks, axis, 0, 0, tiled=False)
    total = jnp.sum(got.astype(jnp.float32), axis=0)
    part = total[: rows // size]
    if extra is not None:
        extra = unpack_rows(total[rows // size:], extra.shape[0] // columns, wire_dtype)
    return part, extra


def exchange_gather(part, axis):
    size = lax.axis_size(axis)
    whole = lax.all_to_all(
        jnp.broadcast_to(part[None], (size,) + part.shape), axis, 0, 0, tiled=False
    )
    return whole.reshape((size * part.shape[0],) + part.shape[1:])


def exchange_sum(x, extra, axis, gather_dtype, wire_dtype=jnp.bfloat16):
    part, extra = exchange_scatter(x, extra, axis, wire_dtype)
    return exchange_gather(part.astype(gather_dtype), axis), extra


def conjugate_gradients(kernel, rhs, n_rows, sample_bits, landmark_bits):
    column_count = rhs.shape[1]
    weights = jnp.zeros_like(rhs)
    residual = rhs
    direction = rhs
    for iteration in range(ITERS):
        if iteration == 0:
            row_part = jnp.dot(kernel, direction.astype(jnp.bfloat16), preferred_element_type=jnp.float32)
            sums = jnp.concatenate(
                [jnp.sum(direction * direction, axis=0), jnp.sum(residual * residual, axis=0)]
            )
            row_chunk, landmark_sums = exchange_scatter(row_part, sums, "landmark", jnp.bfloat16)
            direction_square = landmark_sums[:column_count]
            norm_now = landmark_sums[column_count:]
        else:
            row_part = jnp.dot(kernel, residual.astype(jnp.bfloat16), preferred_element_type=jnp.float32)
            sums = jnp.concatenate(
                [jnp.sum(residual * residual, axis=0), jnp.sum(residual * direction, axis=0)]
            )
            residual_chunk, landmark_sums = exchange_scatter(row_part, sums, "landmark", jnp.bfloat16)
            norm_next = landmark_sums[:column_count]
            cross = landmark_sums[column_count:]
            beta = norm_next / norm_now
            row_chunk = residual_chunk + beta * row_chunk
            direction = residual + beta * direction
            direction_square = norm_next + 2.0 * beta * cross + beta * beta * direction_square
            norm_now = norm_next
        row_half = exchange_gather(row_chunk.astype(jnp.bfloat16), "landmark")
        row_square = jnp.sum(jnp.square(row_half.astype(jnp.float32)), axis=0)
        column_part = jnp.dot(kernel.T, row_half, preferred_element_type=jnp.float32)
        column_total, row_square_total = exchange_sum(
            column_part, row_square, "sample", jnp.float32, jnp.float32
        )
        image = column_total / n_rows + ridge * direction
        curvature = row_square_total / n_rows + ridge * direction_square
        step_size = norm_now / curvature
        weights = weights + step_size * direction
        residual = residual - step_size * image
    return weights, residual


def centred_rhs(raw, targets, n_rows):
    size = lax.axis_size("sample")
    row_count, landmark_count = raw.shape
    column_count = targets.shape[1]
    chunk = landmark_count // size
    column_sum = jnp.sum(raw, axis=0)
    local_mean = column_sum / row_count
    centred = (raw - local_mean[None, :]).astype(jnp.bfloat16)
    product = jnp.dot(centred.T, targets, preferred_element_type=jnp.float32)
    target_sum = jnp.sum(targets.astype(jnp.float32), axis=0)
    payload = jnp.concatenate(
        [
            product.reshape(size, chunk, column_count),
            jnp.broadcast_to(target_sum[None, None, :], (size, 1, column_count)),
            jnp.pad(column_sum.reshape(size, 1, chunk), ((0, 0), (0, 0), (0, column_count - chunk))),
        ],
        axis=1,
    )
    got = lax.all_to_all(payload, "sample", 0, 0, tiled=False)
    target_sums = got[:, chunk, :]
    column_sums = got[:, chunk + 1, :chunk]
    mean_chunk = jnp.sum(column_sums, axis=0) / n_rows
    offsets = column_sums / row_count - mean_chunk[None, :]
    correction = jnp.sum(offsets[:, :, None] * target_sums[:, None, :], axis=0)
    rhs_chunk = (jnp.sum(got[:, :chunk, :], axis=0) + correction) / math.sqrt(n_rows)
    back = jnp.concatenate(
        [rhs_chunk, jnp.pad(mean_chunk[None, :], ((0, 0), (0, column_count - chunk)))], axis=0
    )
    whole = lax.all_to_all(jnp.broadcast_to(back[None], (size,) + back.shape), "sample", 0, 0, tiled=False)
    rhs = whole[:, :chunk, :].reshape(landmark_count, column_count)
    column_mean = whole[:, chunk, :chunk].reshape(landmark_count)
    return rhs, column_mean


def on_device(summaries, row_level, pool, pool_level, landmark_index, level_scale, targets):
    sample_bits = partner_bits(lax.axis_size("sample"), (2, 1, 4, 8, 16, 32, 64))
    landmark_bits = partner_bits(lax.axis_size("landmark"), (1, 2, 4, 8, 16, 32, 64))
    row_count = summaries.shape[0]
    n_rows = row_count * lax.axis_size("sample")
    gathered = lax.all_gather(summaries, "landmark", axis=1, tiled=True)
    feature_count = gathered.shape[1]
    anchors = jnp.take(pool, landmark_index, axis=0)
    anchor_level = jnp.take(pool_level, landmark_index, axis=0)
    row_factor = 1.0 / math.sqrt(feature_count) / level_values(row_level, level_scale)
    anchor_factor = 1.0 / level_values(anchor_level, level_scale)
    raw = raw_block(gathered, row_factor, anchors, anchor_factor)
    rhs, column_mean = centred_rhs(raw, targets, n_rows)
    kernel = (raw - column_mean[None, :]).astype(jnp.bfloat16)
    column_count = targets.shape[1]
    group_width = column_count // GROUPS
    results = [
        conjugate_gradients(
            kernel, rhs[:, g * group_width:(g + 1) * group_width], n_rows, sample_bits, landmark_bits
        )
        for g in range(GROUPS)
    ]
    weights = jnp.concatenate([r[0] for r in results], axis=1)
    residual = jnp.concatenate([r[1] for r in results], axis=1)
    return (weights, residual)


def solution(mesh):
    return jax.shard_map(
        on_device,
        mesh=mesh,
        in_specs=(
            P("sample", "landmark"),
            P("sample"),
            P("landmark", None),
            P("landmark"),
            P("landmark"),
            P(),
            P("sample", None),
        ),
        out_specs=(P("landmark", None), P("landmark", None)),
        check_vma=False,
    )
```

```python
import math

import jax
import jax.numpy as jnp
from jax import lax
from jax.sharding import PartitionSpec as P

ITERS = 2
GROUPS = 1


def REDUCE(x, extra, axis, bits, gather_dtype, wire_dtype=jnp.bfloat16):
    return exchange_sum(x, extra, axis, gather_dtype, wire_dtype)


ridge = 0.5


def level_values(level_ids, level_table):
    onehot = level_ids[:, None] == jnp.arange(level_table.shape[0], dtype=jnp.int32)[None, :]
    return jnp.sum(
        jnp.where(onehot, level_table[None, :], jnp.zeros_like(level_table)[None, :]), axis=1
    )


def raw_block(summary_rows, row_factor, anchors, anchor_factor):
    scores = jnp.dot(summary_rows, anchors.T, preferred_element_type=jnp.float32)
    return jnp.exp(scores * row_factor[:, None] * anchor_factor[None, :])


def partner_bits(size, order):
    bits = [b for b in order if b < size]
    assert sorted(bits) == [1 << i for i in range(size.bit_length() - 1)]
    return bits


def butterfly_sum(x, axis, bits):
    size = lax.axis_size(axis)
    for k in bits:
        perm = [(i, i ^ k) for i in range(size)]
        x = x + lax.ppermute(x, axis, perm)
    return x


def pack_rows(extra, columns, wire_dtype):
    rows = extra.reshape(-1, columns)
    if wire_dtype == jnp.float32:
        parts = [rows]
    else:
        parts = []
        rest = rows
        for _ in range(3):
            term = lax.reduce_precision(rest, exponent_bits=8, mantissa_bits=7)
            parts.append(term)
            rest = rest - term
    return jnp.concatenate(parts, axis=0).astype(wire_dtype)


def unpack_rows(packed, count, wire_dtype):
    terms = 1 if wire_dtype == jnp.float32 else 3
    packed = packed.astype(jnp.float32).reshape(terms, count, -1)
    total = packed[0]
    for t in range(1, terms):
        total = total + packed[t]
    return total.reshape(-1)


def halving_sum(x, extra, axis, bits, gather_dtype, wire_dtype=jnp.bfloat16):
    size = lax.axis_size(axis)
    index = lax.axis_index(axis)
    columns = x.shape[1]
    for k in bits:
        perm = [(i, i ^ k) for i in range(size)]
        half = x.shape[0] // 2
        mine = (index // k) % 2
        keep = lax.dynamic_slice_in_dim(x, mine * half, half, axis=0)
        send = lax.dynamic_slice_in_dim(x, (1 - mine) * half, half, axis=0).astype(wire_dtype)
        if extra is not None:
            send = jnp.concatenate([send, pack_rows(extra, columns, wire_dtype)], axis=0)
        got = lax.ppermute(send, axis, perm)
        x = keep + got[:half].astype(jnp.float32)
        if extra is not None:
            extra = extra + unpack_rows(got[half:], extra.shape[0] // columns, wire_dtype)
    x = x.astype(gather_dtype)
    for k in reversed(bits):
        perm = [(i, i ^ k) for i in range(size)]
        part = x.shape[0]
        mine = (index // k) % 2
        got = lax.ppermute(x, axis, perm)
        whole = jnp.zeros((2 * part,) + x.shape[1:], x.dtype)
        whole = lax.dynamic_update_slice_in_dim(whole, x, mine * part, axis=0)
        x = lax.dynamic_update_slice_in_dim(whole, got, (1 - mine) * part, axis=0)
    return x, extra


def exchange_scatter(x, extra, axis, wire_dtype):
    size = lax.axis_size(axis)
    rows, columns = x.shape
    chunks = x.reshape(size, rows // size, columns).astype(wire_dtype)
    if extra is not None:
        packed = pack_rows(extra, columns, wire_dtype)
        chunks = jnp.concatenate(
            [chunks, jnp.broadcast_to(packed[None], (size,) + packed.shape)], axis=1
        )
    got = lax.all_to_all(chunks, axis, 0, 0, tiled=False)
    total = jnp.sum(got.astype(jnp.float32), axis=0)
    part = total[: rows // size]
    if extra is not None:
        extra = unpack_rows(total[rows // size:], extra.shape[0] // columns, wire_dtype)
    return part, extra


def exchange_gather(part, axis):
    size = lax.axis_size(axis)
    whole = lax.all_to_all(
        jnp.broadcast_to(part[None], (size,) + part.shape), axis, 0, 0, tiled=False
    )
    return whole.reshape((size * part.shape[0],) + part.shape[1:])


def exchange_sum(x, extra, axis, gather_dtype, wire_dtype=jnp.bfloat16):
    part, extra = exchange_scatter(x, extra, axis, wire_dtype)
    return exchange_gather(part.astype(gather_dtype), axis), extra


def native_scatter(x, extra, axis):
    size = lax.axis_size(axis)
    rows, columns = x.shape
    chunks = x.reshape(size, rows // size, columns)
    packed = extra.reshape(-1, columns)
    chunks = jnp.concatenate(
        [chunks, jnp.broadcast_to(packed[None], (size,) + packed.shape)], axis=1
    )
    total = lax.psum_scatter(chunks, axis, scatter_dimension=0, tiled=False)
    return total[: rows // size], total[rows // size:].reshape(-1)


def native_gather(part, axis):
    return lax.all_gather(part, axis, axis=0, tiled=True)


def conjugate_gradients(kernel, targets, n_rows, sample_bits, landmark_bits):
    rhs_part = jnp.dot(kernel.T, targets, preferred_element_type=jnp.float32)
    rhs_total, _ = exchange_sum(rhs_part, None, "sample", jnp.float32, jnp.float32)
    rhs = rhs_total / math.sqrt(n_rows)
    column_count = rhs.shape[1]
    weights = jnp.zeros_like(rhs)
    residual = rhs
    direction = rhs
    for iteration in range(ITERS):
        if iteration == 0:
            row_part = jnp.dot(kernel, direction.astype(jnp.bfloat16), preferred_element_type=jnp.float32)
            sums = jnp.concatenate(
                [jnp.sum(direction * direction, axis=0), jnp.sum(residual * residual, axis=0)]
            )
            row_chunk, landmark_sums = native_scatter(row_part, sums, "landmark")
            direction_square = landmark_sums[:column_count]
            norm_now = landmark_sums[column_count:]
        else:
            row_part = jnp.dot(kernel, residual.astype(jnp.bfloat16), preferred_element_type=jnp.float32)
            sums = jnp.concatenate(
                [jnp.sum(residual * residual, axis=0), jnp.sum(residual * direction, axis=0)]
            )
            residual_chunk, landmark_sums = native_scatter(row_part, sums, "landmark")
            norm_next = landmark_sums[:column_count]
            cross = landmark_sums[column_count:]
            beta = norm_next / norm_now
            row_chunk = residual_chunk + beta * row_chunk
            direction = residual + beta * direction
            direction_square = norm_next + 2.0 * beta * cross + beta * beta * direction_square
            norm_now = norm_next
        row_half = native_gather(row_chunk.astype(jnp.bfloat16), "landmark")
        row_square = jnp.sum(jnp.square(row_half.astype(jnp.float32)), axis=0)
        column_part = jnp.dot(kernel.T, row_half, preferred_element_type=jnp.float32)
        column_total, row_square_total = exchange_sum(
            column_part, row_square, "sample", jnp.float32, jnp.float32
        )
        image = column_total / n_rows + ridge * direction
        curvature = row_square_total / n_rows + ridge * direction_square
        step_size = norm_now / curvature
        weights = weights + step_size * direction
        residual = residual - step_size * image
    return weights, residual


def on_device(summaries, row_level, pool, pool_level, landmark_index, level_scale, targets):
    sample_bits = partner_bits(lax.axis_size("sample"), (2, 1, 4, 8, 16, 32, 64))
    landmark_bits = partner_bits(lax.axis_size("landmark"), (1, 2, 4, 8, 16, 32, 64))
    row_count = summaries.shape[0]
    n_rows = row_count * lax.axis_size("sample")
    gathered = lax.all_gather(summaries, "landmark", axis=1, tiled=True)
    feature_count = gathered.shape[1]
    anchors = jnp.take(pool, landmark_index, axis=0)
    anchor_level = jnp.take(pool_level, landmark_index, axis=0)
    row_factor = 1.0 / math.sqrt(feature_count) / level_values(row_level, level_scale)
    anchor_factor = 1.0 / level_values(anchor_level, level_scale)
    raw = raw_block(gathered, row_factor, anchors, anchor_factor)
    column_mean = butterfly_sum(jnp.sum(raw, axis=0), "sample", sample_bits) / n_rows
    kernel = (raw - column_mean[None, :]).astype(jnp.bfloat16)
    column_count = targets.shape[1]
    group_width = column_count // GROUPS
    results = [
        conjugate_gradients(
            kernel, targets[:, g * group_width:(g + 1) * group_width], n_rows, sample_bits, landmark_bits
        )
        for g in range(GROUPS)
    ]
    weights = jnp.concatenate([r[0] for r in results], axis=1)
    residual = jnp.concatenate([r[1] for r in results], axis=1)
    return (weights, residual)


def solution(mesh):
    return jax.shard_map(
        on_device,
        mesh=mesh,
        in_specs=(
            P("sample", "landmark"),
            P("sample"),
            P("landmark", None),
            P("landmark"),
            P("landmark"),
            P(),
            P("sample", None),
        ),
        out_specs=(P("landmark", None), P("landmark", None)),
        check_vma=False,
    )
```

```python
import math

import jax
import jax.numpy as jnp
from jax import lax
from jax.sharding import PartitionSpec as P

ITERS = 2
GROUPS = 1


def REDUCE(x, extra, axis, bits, gather_dtype, wire_dtype=jnp.bfloat16):
    return exchange_sum(x, extra, axis, gather_dtype, wire_dtype)


ridge = 0.5


def level_values(level_ids, level_table):
    onehot = level_ids[:, None] == jnp.arange(level_table.shape[0], dtype=jnp.int32)[None, :]
    return jnp.sum(
        jnp.where(onehot, level_table[None, :], jnp.zeros_like(level_table)[None, :]), axis=1
    )


def raw_block(summary_rows, row_factor, anchors, anchor_factor):
    scores = jnp.dot(summary_rows, anchors.T, preferred_element_type=jnp.float32)
    return jnp.exp(scores * row_factor[:, None] * anchor_factor[None, :])


def partner_bits(size, order):
    bits = [b for b in order if b < size]
    assert sorted(bits) == [1 << i for i in range(size.bit_length() - 1)]
    return bits


def butterfly_sum(x, axis, bits):
    size = lax.axis_size(axis)
    for k in bits:
        perm = [(i, i ^ k) for i in range(size)]
        x = x + lax.ppermute(x, axis, perm)
    return x


def pack_rows(extra, columns, wire_dtype):
    rows = extra.reshape(-1, columns)
    if wire_dtype == jnp.float32:
        parts = [rows]
    else:
        parts = []
        rest = rows
        for _ in range(3):
            term = lax.reduce_precision(rest, exponent_bits=8, mantissa_bits=7)
            parts.append(term)
            rest = rest - term
    return jnp.concatenate(parts, axis=0).astype(wire_dtype)


def unpack_rows(packed, count, wire_dtype):
    terms = 1 if wire_dtype == jnp.float32 else 3
    packed = packed.astype(jnp.float32).reshape(terms, count, -1)
    total = packed[0]
    for t in range(1, terms):
        total = total + packed[t]
    return total.reshape(-1)


def halving_sum(x, extra, axis, bits, gather_dtype, wire_dtype=jnp.bfloat16):
    size = lax.axis_size(axis)
    index = lax.axis_index(axis)
    columns = x.shape[1]
    for k in bits:
        perm = [(i, i ^ k) for i in range(size)]
        half = x.shape[0] // 2
        mine = (index // k) % 2
        keep = lax.dynamic_slice_in_dim(x, mine * half, half, axis=0)
        send = lax.dynamic_slice_in_dim(x, (1 - mine) * half, half, axis=0).astype(wire_dtype)
        if extra is not None:
            send = jnp.concatenate([send, pack_rows(extra, columns, wire_dtype)], axis=0)
        got = lax.ppermute(send, axis, perm)
        x = keep + got[:half].astype(jnp.float32)
        if extra is not None:
            extra = extra + unpack_rows(got[half:], extra.shape[0] // columns, wire_dtype)
    x = x.astype(gather_dtype)
    for k in reversed(bits):
        perm = [(i, i ^ k) for i in range(size)]
        part = x.shape[0]
        mine = (index // k) % 2
        got = lax.ppermute(x, axis, perm)
        whole = jnp.zeros((2 * part,) + x.shape[1:], x.dtype)
        whole = lax.dynamic_update_slice_in_dim(whole, x, mine * part, axis=0)
        x = lax.dynamic_update_slice_in_dim(whole, got, (1 - mine) * part, axis=0)
    return x, extra


def exchange_scatter(x, extra, axis, wire_dtype):
    size = lax.axis_size(axis)
    rows, columns = x.shape
    chunks = x.reshape(size, rows // size, columns).astype(wire_dtype)
    if extra is not None:
        packed = pack_rows(extra, columns, wire_dtype)
        chunks = jnp.concatenate(
            [chunks, jnp.broadcast_to(packed[None], (size,) + packed.shape)], axis=1
        )
    got = lax.all_to_all(chunks, axis, 0, 0, tiled=False)
    total = jnp.sum(got.astype(jnp.float32), axis=0)
    part = total[: rows // size]
    if extra is not None:
        extra = unpack_rows(total[rows // size:], extra.shape[0] // columns, wire_dtype)
    return part, extra


def exchange_gather(part, axis):
    size = lax.axis_size(axis)
    whole = lax.all_to_all(
        jnp.broadcast_to(part[None], (size,) + part.shape), axis, 0, 0, tiled=False
    )
    return whole.reshape((size * part.shape[0],) + part.shape[1:])


def exchange_sum(x, extra, axis, gather_dtype, wire_dtype=jnp.bfloat16):
    part, extra = exchange_scatter(x, extra, axis, wire_dtype)
    return exchange_gather(part.astype(gather_dtype), axis), extra


def conjugate_gradients(kernel, targets, n_rows, sample_bits, landmark_bits):
    rhs_part = jnp.dot(kernel.T, targets, preferred_element_type=jnp.float32)
    rhs_total, _ = exchange_sum(rhs_part, None, "sample", jnp.float32, jnp.float32)
    rhs = rhs_total / math.sqrt(n_rows)
    column_count = rhs.shape[1]
    weights = jnp.zeros_like(rhs)
    residual = rhs
    direction = rhs
    for iteration in range(ITERS):
        if iteration == 0:
            row_part = jnp.dot(kernel, direction.astype(jnp.bfloat16), preferred_element_type=jnp.float32)
            sums = jnp.concatenate(
                [jnp.sum(direction * direction, axis=0), jnp.sum(residual * residual, axis=0)]
            )
            row_chunk, landmark_sums = exchange_scatter(row_part, sums, "landmark", jnp.bfloat16)
            direction_square = landmark_sums[:column_count]
            norm_now = landmark_sums[column_count:]
        else:
            row_part = jnp.dot(kernel, residual.astype(jnp.bfloat16), preferred_element_type=jnp.float32)
            sums = jnp.concatenate(
                [jnp.sum(residual * residual, axis=0), jnp.sum(residual * direction, axis=0)]
            )
            residual_chunk, landmark_sums = exchange_scatter(row_part, sums, "landmark", jnp.bfloat16)
            norm_next = landmark_sums[:column_count]
            cross = landmark_sums[column_count:]
            beta = norm_next / norm_now
            row_chunk = residual_chunk + beta * row_chunk
            direction = residual + beta * direction
            direction_square = norm_next + 2.0 * beta * cross + beta * beta * direction_square
            norm_now = norm_next
        row_half = exchange_gather(row_chunk.astype(jnp.bfloat16), "landmark")
        row_square = jnp.sum(jnp.square(row_half.astype(jnp.float32)), axis=0)
        column_part = jnp.dot(kernel.T, row_half, preferred_element_type=jnp.float32)
        column_total, row_square_total = exchange_sum(
            column_part, row_square, "sample", jnp.float32, jnp.float32
        )
        image = column_total / n_rows + ridge * direction
        curvature = row_square_total / n_rows + ridge * direction_square
        step_size = norm_now / curvature
        weights = weights + step_size * direction
        residual = residual - step_size * image
    return weights, residual


def on_device(summaries, row_level, pool, pool_level, landmark_index, level_scale, targets):
    sample_bits = partner_bits(lax.axis_size("sample"), (2, 1, 4, 8, 16, 32, 64))
    landmark_bits = partner_bits(lax.axis_size("landmark"), (1, 2, 4, 8, 16, 32, 64))
    row_count = summaries.shape[0]
    n_rows = row_count * lax.axis_size("sample")
    gathered = lax.all_gather(summaries, "landmark", axis=1, tiled=True)
    feature_count = gathered.shape[1]
    anchors = jnp.take(pool, landmark_index, axis=0)
    anchor_level = jnp.take(pool_level, landmark_index, axis=0)
    row_factor = 1.0 / math.sqrt(feature_count) / level_values(row_level, level_scale)
    anchor_factor = 1.0 / level_values(anchor_level, level_scale)
    kernel_parts = []
    half = anchors.shape[0] // 2
    for h in range(2):
        raw = raw_block(gathered, row_factor, anchors[h * half:(h + 1) * half], anchor_factor[h * half:(h + 1) * half])
        column_mean = butterfly_sum(jnp.sum(raw, axis=0), "sample", sample_bits) / n_rows
        kernel_parts.append((raw - column_mean[None, :]).astype(jnp.bfloat16))
    kernel = jnp.concatenate(kernel_parts, axis=1)
    column_count = targets.shape[1]
    group_width = column_count // GROUPS
    results = [
        conjugate_gradients(
            kernel, targets[:, g * group_width:(g + 1) * group_width], n_rows, sample_bits, landmark_bits
        )
        for g in range(GROUPS)
    ]
    weights = jnp.concatenate([r[0] for r in results], axis=1)
    residual = jnp.concatenate([r[1] for r in results], axis=1)
    return (weights, residual)


def solution(mesh):
    return jax.shard_map(
        on_device,
        mesh=mesh,
        in_specs=(
            P("sample", "landmark"),
            P("sample"),
            P("landmark", None),
            P("landmark"),
            P("landmark"),
            P(),
            P("sample", None),
        ),
        out_specs=(P("landmark", None), P("landmark", None)),
        check_vma=False,
    )
```

```python
import math

import jax
import jax.numpy as jnp
from jax import lax
from jax.sharding import PartitionSpec as P

ITERS = 2
GROUPS = 1


def REDUCE(x, extra, axis, bits, gather_dtype, wire_dtype=jnp.bfloat16):
    return exchange_sum(x, extra, axis, gather_dtype, wire_dtype)


ridge = 0.5


def level_values(level_ids, level_table):
    onehot = level_ids[:, None] == jnp.arange(level_table.shape[0], dtype=jnp.int32)[None, :]
    return jnp.sum(
        jnp.where(onehot, level_table[None, :], jnp.zeros_like(level_table)[None, :]), axis=1
    )


def raw_block(summary_rows, row_factor, anchors, anchor_factor):
    scores = jnp.dot(summary_rows, anchors.T, preferred_element_type=jnp.float32)
    return jnp.exp(scores * row_factor[:, None] * anchor_factor[None, :])


def partner_bits(size, order):
    bits = [b for b in order if b < size]
    assert sorted(bits) == [1 << i for i in range(size.bit_length() - 1)]
    return bits


def butterfly_sum(x, axis, bits):
    size = lax.axis_size(axis)
    for k in bits:
        perm = [(i, i ^ k) for i in range(size)]
        x = x + lax.ppermute(x, axis, perm)
    return x


def pack_rows(extra, columns, wire_dtype):
    rows = extra.reshape(-1, columns)
    if wire_dtype == jnp.float32:
        parts = [rows]
    else:
        parts = []
        rest = rows
        for _ in range(3):
            term = lax.reduce_precision(rest, exponent_bits=8, mantissa_bits=7)
            parts.append(term)
            rest = rest - term
    return jnp.concatenate(parts, axis=0).astype(wire_dtype)


def unpack_rows(packed, count, wire_dtype):
    terms = 1 if wire_dtype == jnp.float32 else 3
    packed = packed.astype(jnp.float32).reshape(terms, count, -1)
    total = packed[0]
    for t in range(1, terms):
        total = total + packed[t]
    return total.reshape(-1)


def halving_sum(x, extra, axis, bits, gather_dtype, wire_dtype=jnp.bfloat16):
    size = lax.axis_size(axis)
    index = lax.axis_index(axis)
    columns = x.shape[1]
    for k in bits:
        perm = [(i, i ^ k) for i in range(size)]
        half = x.shape[0] // 2
        mine = (index // k) % 2
        keep = lax.dynamic_slice_in_dim(x, mine * half, half, axis=0)
        send = lax.dynamic_slice_in_dim(x, (1 - mine) * half, half, axis=0).astype(wire_dtype)
        if extra is not None:
            send = jnp.concatenate([send, pack_rows(extra, columns, wire_dtype)], axis=0)
        got = lax.ppermute(send, axis, perm)
        x = keep + got[:half].astype(jnp.float32)
        if extra is not None:
            extra = extra + unpack_rows(got[half:], extra.shape[0] // columns, wire_dtype)
    x = x.astype(gather_dtype)
    for k in reversed(bits):
        perm = [(i, i ^ k) for i in range(size)]
        part = x.shape[0]
        mine = (index // k) % 2
        got = lax.ppermute(x, axis, perm)
        whole = jnp.zeros((2 * part,) + x.shape[1:], x.dtype)
        whole = lax.dynamic_update_slice_in_dim(whole, x, mine * part, axis=0)
        x = lax.dynamic_update_slice_in_dim(whole, got, (1 - mine) * part, axis=0)
    return x, extra


def exchange_scatter(x, extra, axis, wire_dtype):
    size = lax.axis_size(axis)
    rows, columns = x.shape
    chunks = x.reshape(size, rows // size, columns).astype(wire_dtype)
    if extra is not None:
        packed = pack_rows(extra, columns, wire_dtype)
        chunks = jnp.concatenate(
            [chunks, jnp.broadcast_to(packed[None], (size,) + packed.shape)], axis=1
        )
    got = lax.all_to_all(chunks, axis, 0, 0, tiled=False)
    total = jnp.sum(got.astype(jnp.float32), axis=0)
    part = total[: rows // size]
    if extra is not None:
        extra = unpack_rows(total[rows // size:], extra.shape[0] // columns, wire_dtype)
    return part, extra


def exchange_gather(part, axis):
    size = lax.axis_size(axis)
    whole = lax.all_to_all(
        jnp.broadcast_to(part[None], (size,) + part.shape), axis, 0, 0, tiled=False
    )
    return whole.reshape((size * part.shape[0],) + part.shape[1:])


def exchange_sum(x, extra, axis, gather_dtype, wire_dtype=jnp.bfloat16):
    part, extra = exchange_scatter(x, extra, axis, wire_dtype)
    return exchange_gather(part.astype(gather_dtype), axis), extra


def conjugate_gradients(kernel, targets, n_rows, sample_bits, landmark_bits):
    rhs_part = jnp.dot(kernel.T, targets, preferred_element_type=jnp.float32)
    rhs_total, _ = exchange_sum(rhs_part, None, "sample", jnp.float32, jnp.float32)
    rhs = rhs_total / math.sqrt(n_rows)
    column_count = rhs.shape[1]
    weights = jnp.zeros_like(rhs)
    residual = rhs
    direction = rhs
    for iteration in range(ITERS):
        if iteration == 0:
            row_part = jnp.dot(kernel, direction.astype(jnp.bfloat16), preferred_element_type=jnp.float32)
            sums = jnp.concatenate(
                [jnp.sum(direction * direction, axis=0), jnp.sum(residual * residual, axis=0)]
            )
            row_chunk, landmark_sums = exchange_scatter(row_part, sums, "landmark", jnp.bfloat16)
            direction_square = landmark_sums[:column_count]
            norm_now = landmark_sums[column_count:]
        else:
            row_part = jnp.dot(kernel, residual.astype(jnp.bfloat16), preferred_element_type=jnp.float32)
            sums = jnp.concatenate(
                [jnp.sum(residual * residual, axis=0), jnp.sum(residual * direction, axis=0)]
            )
            residual_chunk, landmark_sums = exchange_scatter(row_part, sums, "landmark", jnp.bfloat16)
            norm_next = landmark_sums[:column_count]
            cross = landmark_sums[column_count:]
            beta = norm_next / norm_now
            row_chunk = residual_chunk + beta * row_chunk
            direction = residual + beta * direction
            direction_square = norm_next + 2.0 * beta * cross + beta * beta * direction_square
            norm_now = norm_next
        row_half = exchange_gather(row_chunk.astype(jnp.bfloat16), "landmark")
        row_square = jnp.sum(jnp.square(row_half.astype(jnp.float32)), axis=0)
        column_part = jnp.dot(kernel.T, row_half, preferred_element_type=jnp.float32)
        column_total, row_square_total = exchange_sum(
            column_part, row_square, "sample", jnp.float32, jnp.float32
        )
        image = column_total / n_rows + ridge * direction
        curvature = row_square_total / n_rows + ridge * direction_square
        step_size = norm_now / curvature
        weights = weights + step_size * direction
        residual = residual - step_size * image
    return weights, residual


def gather_sum(x, axis):
    size = lax.axis_size(axis)
    index = lax.axis_index(axis)
    copies = [x] + [
        lax.ppermute(x, axis, [(i, (i + shift) % size) for i in range(size)])
        for shift in range(1, size)
    ]
    stacked = jnp.stack(copies)
    ordered = jnp.take(stacked, (index - jnp.arange(size)) % size, axis=0)
    total = ordered[0]
    for j in range(1, size):
        total = total + ordered[j]
    return total


def on_device(summaries, row_level, pool, pool_level, landmark_index, level_scale, targets):
    sample_bits = partner_bits(lax.axis_size("sample"), (2, 1, 4, 8, 16, 32, 64))
    landmark_bits = partner_bits(lax.axis_size("landmark"), (1, 2, 4, 8, 16, 32, 64))
    row_count = summaries.shape[0]
    n_rows = row_count * lax.axis_size("sample")
    gathered = lax.all_gather(summaries, "landmark", axis=1, tiled=True)
    feature_count = gathered.shape[1]
    anchors = jnp.take(pool, landmark_index, axis=0)
    anchor_level = jnp.take(pool_level, landmark_index, axis=0)
    row_factor = 1.0 / math.sqrt(feature_count) / level_values(row_level, level_scale)
    anchor_factor = 1.0 / level_values(anchor_level, level_scale)
    raw = raw_block(gathered, row_factor, anchors, anchor_factor)
    column_mean = gather_sum(jnp.sum(raw, axis=0), "sample") / n_rows
    kernel = (raw - column_mean[None, :]).astype(jnp.bfloat16)
    column_count = targets.shape[1]
    group_width = column_count // GROUPS
    results = [
        conjugate_gradients(
            kernel, targets[:, g * group_width:(g + 1) * group_width], n_rows, sample_bits, landmark_bits
        )
        for g in range(GROUPS)
    ]
    weights = jnp.concatenate([r[0] for r in results], axis=1)
    residual = jnp.concatenate([r[1] for r in results], axis=1)
    return (weights, residual)


def solution(mesh):
    return jax.shard_map(
        on_device,
        mesh=mesh,
        in_specs=(
            P("sample", "landmark"),
            P("sample"),
            P("landmark", None),
            P("landmark"),
            P("landmark"),
            P(),
            P("sample", None),
        ),
        out_specs=(P("landmark", None), P("landmark", None)),
        check_vma=False,
    )
```

```python
import math

import jax
import jax.numpy as jnp
from jax import lax
from jax.sharding import PartitionSpec as P

ITERS = 2
GROUPS = 1


def REDUCE(x, extra, axis, bits, gather_dtype, wire_dtype=jnp.bfloat16):
    return exchange_sum(x, extra, axis, gather_dtype, wire_dtype)


ridge = 0.5


def level_values(level_ids, level_table):
    onehot = level_ids[:, None] == jnp.arange(level_table.shape[0], dtype=jnp.int32)[None, :]
    return jnp.sum(
        jnp.where(onehot, level_table[None, :], jnp.zeros_like(level_table)[None, :]), axis=1
    )


def raw_block(summary_rows, row_factor, anchors, anchor_factor):
    scores = jnp.dot(summary_rows, anchors.T, preferred_element_type=jnp.float32)
    return jnp.exp(scores * row_factor[:, None] * anchor_factor[None, :])


def partner_bits(size, order):
    bits = [b for b in order if b < size]
    assert sorted(bits) == [1 << i for i in range(size.bit_length() - 1)]
    return bits


def butterfly_sum(x, axis, bits):
    size = lax.axis_size(axis)
    for k in bits:
        perm = [(i, i ^ k) for i in range(size)]
        x = x + lax.ppermute(x, axis, perm)
    return x


def pack_rows(extra, columns, wire_dtype):
    rows = extra.reshape(-1, columns)
    if wire_dtype == jnp.float32:
        parts = [rows]
    else:
        parts = []
        rest = rows
        for _ in range(3):
            term = lax.reduce_precision(rest, exponent_bits=8, mantissa_bits=7)
            parts.append(term)
            rest = rest - term
    return jnp.concatenate(parts, axis=0).astype(wire_dtype)


def unpack_rows(packed, count, wire_dtype):
    terms = 1 if wire_dtype == jnp.float32 else 3
    packed = packed.astype(jnp.float32).reshape(terms, count, -1)
    total = packed[0]
    for t in range(1, terms):
        total = total + packed[t]
    return total.reshape(-1)


def halving_sum(x, extra, axis, bits, gather_dtype, wire_dtype=jnp.bfloat16):
    size = lax.axis_size(axis)
    index = lax.axis_index(axis)
    columns = x.shape[1]
    for k in bits:
        perm = [(i, i ^ k) for i in range(size)]
        half = x.shape[0] // 2
        mine = (index // k) % 2
        keep = lax.dynamic_slice_in_dim(x, mine * half, half, axis=0)
        send = lax.dynamic_slice_in_dim(x, (1 - mine) * half, half, axis=0).astype(wire_dtype)
        if extra is not None:
            send = jnp.concatenate([send, pack_rows(extra, columns, wire_dtype)], axis=0)
        got = lax.ppermute(send, axis, perm)
        x = keep + got[:half].astype(jnp.float32)
        if extra is not None:
            extra = extra + unpack_rows(got[half:], extra.shape[0] // columns, wire_dtype)
    x = x.astype(gather_dtype)
    for k in reversed(bits):
        perm = [(i, i ^ k) for i in range(size)]
        part = x.shape[0]
        mine = (index // k) % 2
        got = lax.ppermute(x, axis, perm)
        whole = jnp.zeros((2 * part,) + x.shape[1:], x.dtype)
        whole = lax.dynamic_update_slice_in_dim(whole, x, mine * part, axis=0)
        x = lax.dynamic_update_slice_in_dim(whole, got, (1 - mine) * part, axis=0)
    return x, extra


def exchange_scatter(x, extra, axis, wire_dtype):
    size = lax.axis_size(axis)
    rows, columns = x.shape
    chunks = x.reshape(size, rows // size, columns).astype(wire_dtype)
    if extra is not None:
        packed = pack_rows(extra, columns, wire_dtype)
        chunks = jnp.concatenate(
            [chunks, jnp.broadcast_to(packed[None], (size,) + packed.shape)], axis=1
        )
    got = lax.all_to_all(chunks, axis, 0, 0, tiled=False)
    total = jnp.sum(got.astype(jnp.float32), axis=0)
    part = total[: rows // size]
    if extra is not None:
        extra = unpack_rows(total[rows // size:], extra.shape[0] // columns, wire_dtype)
    return part, extra


def exchange_gather(part, axis):
    size = lax.axis_size(axis)
    whole = lax.all_to_all(
        jnp.broadcast_to(part[None], (size,) + part.shape), axis, 0, 0, tiled=False
    )
    return whole.reshape((size * part.shape[0],) + part.shape[1:])


def exchange_sum(x, extra, axis, gather_dtype, wire_dtype=jnp.bfloat16):
    part, extra = exchange_scatter(x, extra, axis, wire_dtype)
    return exchange_gather(part.astype(gather_dtype), axis), extra


def conjugate_gradients(kernel, targets, n_rows, sample_bits, landmark_bits):
    rhs_part = jnp.dot(kernel.T, targets, preferred_element_type=jnp.float32)
    rhs_total, _ = exchange_sum(rhs_part, None, "sample", jnp.float32, jnp.float32)
    rhs = rhs_total / math.sqrt(n_rows)
    column_count = rhs.shape[1]
    weights = jnp.zeros_like(rhs)
    residual = rhs
    direction = rhs
    for iteration in range(ITERS):
        if iteration == 0:
            row_part = jnp.dot(kernel, direction.astype(jnp.bfloat16), preferred_element_type=jnp.float32)
            sums = jnp.concatenate(
                [jnp.sum(direction * direction, axis=0), jnp.sum(residual * residual, axis=0)]
            )
            row_chunk, landmark_sums = exchange_scatter(row_part, sums, "landmark", jnp.bfloat16)
            direction_square = landmark_sums[:column_count]
            norm_now = landmark_sums[column_count:]
        else:
            row_part = jnp.dot(kernel, residual.astype(jnp.bfloat16), preferred_element_type=jnp.float32)
            sums = jnp.concatenate(
                [jnp.sum(residual * residual, axis=0), jnp.sum(residual * direction, axis=0)]
            )
            residual_chunk, landmark_sums = exchange_scatter(row_part, sums, "landmark", jnp.bfloat16)
            norm_next = landmark_sums[:column_count]
            cross = landmark_sums[column_count:]
            beta = norm_next / norm_now
            row_chunk = residual_chunk + beta * row_chunk
            direction = residual + beta * direction
            direction_square = norm_next + 2.0 * beta * cross + beta * beta * direction_square
            norm_now = norm_next
        row_half = exchange_gather(row_chunk.astype(jnp.bfloat16), "landmark")
        row_square = jnp.sum(jnp.square(row_half.astype(jnp.float32)), axis=0)
        column_part = jnp.dot(kernel.T, row_half, preferred_element_type=jnp.float32)
        column_chunk, row_square_total = exchange_scatter(
            column_part, row_square, "sample", jnp.float32
        )
        curvature = row_square_total / n_rows + ridge * direction_square
        step_size = norm_now / curvature
        weights = weights + step_size * direction
        residual = residual - (step_size * ridge) * direction
        column_total = exchange_gather(column_chunk, "sample")
        residual = residual - (step_size / n_rows) * column_total
    return weights, residual


def on_device(summaries, row_level, pool, pool_level, landmark_index, level_scale, targets):
    sample_bits = partner_bits(lax.axis_size("sample"), (2, 1, 4, 8, 16, 32, 64))
    landmark_bits = partner_bits(lax.axis_size("landmark"), (1, 2, 4, 8, 16, 32, 64))
    row_count = summaries.shape[0]
    n_rows = row_count * lax.axis_size("sample")
    gathered = lax.all_gather(summaries, "landmark", axis=1, tiled=True)
    feature_count = gathered.shape[1]
    anchors = jnp.take(pool, landmark_index, axis=0)
    anchor_level = jnp.take(pool_level, landmark_index, axis=0)
    row_factor = 1.0 / math.sqrt(feature_count) / level_values(row_level, level_scale)
    anchor_factor = 1.0 / level_values(anchor_level, level_scale)
    raw = raw_block(gathered, row_factor, anchors, anchor_factor)
    column_mean = butterfly_sum(jnp.sum(raw, axis=0), "sample", sample_bits) / n_rows
    kernel = (raw - column_mean[None, :]).astype(jnp.bfloat16)
    column_count = targets.shape[1]
    group_width = column_count // GROUPS
    results = [
        conjugate_gradients(
            kernel, targets[:, g * group_width:(g + 1) * group_width], n_rows, sample_bits, landmark_bits
        )
        for g in range(GROUPS)
    ]
    weights = jnp.concatenate([r[0] for r in results], axis=1)
    residual = jnp.concatenate([r[1] for r in results], axis=1)
    return (weights, residual)


def solution(mesh):
    return jax.shard_map(
        on_device,
        mesh=mesh,
        in_specs=(
            P("sample", "landmark"),
            P("sample"),
            P("landmark", None),
            P("landmark"),
            P("landmark"),
            P(),
            P("sample", None),
        ),
        out_specs=(P("landmark", None), P("landmark", None)),
        check_vma=False,
    )
```

```python
import math

import jax
import jax.numpy as jnp
from jax import lax
from jax.sharding import PartitionSpec as P

ITERS = 2
GROUPS = 1


def REDUCE(x, extra, axis, bits, gather_dtype, wire_dtype=jnp.bfloat16):
    return exchange_sum(x, extra, axis, gather_dtype, wire_dtype)


ridge = 0.5


def level_values(level_ids, level_table):
    onehot = level_ids[:, None] == jnp.arange(level_table.shape[0], dtype=jnp.int32)[None, :]
    return jnp.sum(
        jnp.where(onehot, level_table[None, :], jnp.zeros_like(level_table)[None, :]), axis=1
    )


def raw_block(summary_rows, row_factor, anchors, anchor_factor):
    scores = jnp.dot(summary_rows, anchors.T, preferred_element_type=jnp.float32)
    return jnp.exp(scores * row_factor[:, None] * anchor_factor[None, :])


def partner_bits(size, order):
    bits = [b for b in order if b < size]
    assert sorted(bits) == [1 << i for i in range(size.bit_length() - 1)]
    return bits


def butterfly_sum(x, axis, bits):
    size = lax.axis_size(axis)
    for k in bits:
        perm = [(i, i ^ k) for i in range(size)]
        x = x + lax.ppermute(x, axis, perm)
    return x


def pack_rows(extra, columns, wire_dtype):
    rows = extra.reshape(-1, columns)
    if wire_dtype == jnp.float32:
        parts = [rows]
    else:
        parts = []
        rest = rows
        for _ in range(3):
            term = lax.reduce_precision(rest, exponent_bits=8, mantissa_bits=7)
            parts.append(term)
            rest = rest - term
    return jnp.concatenate(parts, axis=0).astype(wire_dtype)


def unpack_rows(packed, count, wire_dtype):
    terms = 1 if wire_dtype == jnp.float32 else 3
    packed = packed.astype(jnp.float32).reshape(terms, count, -1)
    total = packed[0]
    for t in range(1, terms):
        total = total + packed[t]
    return total.reshape(-1)


def halving_sum(x, extra, axis, bits, gather_dtype, wire_dtype=jnp.bfloat16):
    size = lax.axis_size(axis)
    index = lax.axis_index(axis)
    columns = x.shape[1]
    for k in bits:
        perm = [(i, i ^ k) for i in range(size)]
        half = x.shape[0] // 2
        mine = (index // k) % 2
        keep = lax.dynamic_slice_in_dim(x, mine * half, half, axis=0)
        send = lax.dynamic_slice_in_dim(x, (1 - mine) * half, half, axis=0).astype(wire_dtype)
        if extra is not None:
            send = jnp.concatenate([send, pack_rows(extra, columns, wire_dtype)], axis=0)
        got = lax.ppermute(send, axis, perm)
        x = keep + got[:half].astype(jnp.float32)
        if extra is not None:
            extra = extra + unpack_rows(got[half:], extra.shape[0] // columns, wire_dtype)
    x = x.astype(gather_dtype)
    for k in reversed(bits):
        perm = [(i, i ^ k) for i in range(size)]
        part = x.shape[0]
        mine = (index // k) % 2
        got = lax.ppermute(x, axis, perm)
        whole = jnp.zeros((2 * part,) + x.shape[1:], x.dtype)
        whole = lax.dynamic_update_slice_in_dim(whole, x, mine * part, axis=0)
        x = lax.dynamic_update_slice_in_dim(whole, got, (1 - mine) * part, axis=0)
    return x, extra


def exchange_scatter(x, extra, axis, wire_dtype):
    size = lax.axis_size(axis)
    rows, columns = x.shape
    chunks = x.reshape(size, rows // size, columns).astype(wire_dtype)
    if extra is not None:
        packed = pack_rows(extra, columns, wire_dtype)
        chunks = jnp.concatenate(
            [chunks, jnp.broadcast_to(packed[None], (size,) + packed.shape)], axis=1
        )
    got = lax.all_to_all(chunks, axis, 0, 0, tiled=False)
    total = jnp.sum(got.astype(jnp.float32), axis=0)
    part = total[: rows // size]
    if extra is not None:
        extra = unpack_rows(total[rows // size:], extra.shape[0] // columns, wire_dtype)
    return part, extra


def exchange_gather(part, axis):
    size = lax.axis_size(axis)
    whole = lax.all_to_all(
        jnp.broadcast_to(part[None], (size,) + part.shape), axis, 0, 0, tiled=False
    )
    return whole.reshape((size * part.shape[0],) + part.shape[1:])


def exchange_sum(x, extra, axis, gather_dtype, wire_dtype=jnp.bfloat16):
    part, extra = exchange_scatter(x, extra, axis, wire_dtype)
    return exchange_gather(part.astype(gather_dtype), axis), extra


def conjugate_gradients(kernel, targets, n_rows, sample_bits, landmark_bits):
    rhs_part = jnp.dot(kernel.T, targets, preferred_element_type=jnp.float32)
    rhs_total, _ = exchange_sum(rhs_part, None, "sample", jnp.float32, jnp.float32)
    rhs = rhs_total / math.sqrt(n_rows)
    column_count = rhs.shape[1]
    weights = jnp.zeros_like(rhs)
    residual = rhs
    direction = rhs
    for iteration in range(ITERS):
        if iteration == 0:
            row_part = jnp.dot(kernel, direction.astype(jnp.bfloat16), preferred_element_type=jnp.float32)
            sums = jnp.concatenate(
                [jnp.sum(direction * direction, axis=0), jnp.sum(residual * residual, axis=0)]
            )
            row_chunk, landmark_sums = exchange_scatter(row_part, sums, "landmark", jnp.bfloat16)
            direction_square = landmark_sums[:column_count]
            norm_now = landmark_sums[column_count:]
        else:
            row_part = jnp.dot(kernel, residual.astype(jnp.bfloat16), preferred_element_type=jnp.float32)
            sums = jnp.concatenate(
                [jnp.sum(residual * residual, axis=0), jnp.sum(residual * direction, axis=0)]
            )
            residual_chunk, landmark_sums = exchange_scatter(row_part, sums, "landmark", jnp.bfloat16)
            norm_next = landmark_sums[:column_count]
            cross = landmark_sums[column_count:]
            beta = norm_next / norm_now
            row_chunk = residual_chunk + beta * row_chunk
            direction = residual + beta * direction
            direction_square = norm_next + 2.0 * beta * cross + beta * beta * direction_square
            norm_now = norm_next
        row_half = lax.all_gather(row_chunk.astype(jnp.bfloat16), "landmark", axis=0, tiled=True)
        row_square = jnp.sum(jnp.square(row_half.astype(jnp.float32)), axis=0)
        column_part = jnp.dot(kernel.T, row_half, preferred_element_type=jnp.float32)
        column_total, row_square_total = exchange_sum(
            column_part, row_square, "sample", jnp.float32, jnp.float32
        )
        image = column_total / n_rows + ridge * direction
        curvature = row_square_total / n_rows + ridge * direction_square
        step_size = norm_now / curvature
        weights = weights + step_size * direction
        residual = residual - step_size * image
    return weights, residual


def on_device(summaries, row_level, pool, pool_level, landmark_index, level_scale, targets):
    sample_bits = partner_bits(lax.axis_size("sample"), (2, 1, 4, 8, 16, 32, 64))
    landmark_bits = partner_bits(lax.axis_size("landmark"), (1, 2, 4, 8, 16, 32, 64))
    row_count = summaries.shape[0]
    n_rows = row_count * lax.axis_size("sample")
    gathered = lax.all_gather(summaries, "landmark", axis=1, tiled=True)
    feature_count = gathered.shape[1]
    anchors = jnp.take(pool, landmark_index, axis=0)
    anchor_level = jnp.take(pool_level, landmark_index, axis=0)
    row_factor = 1.0 / math.sqrt(feature_count) / level_values(row_level, level_scale)
    anchor_factor = 1.0 / level_values(anchor_level, level_scale)
    raw = raw_block(gathered, row_factor, anchors, anchor_factor)
    column_mean = butterfly_sum(jnp.sum(raw, axis=0), "sample", sample_bits) / n_rows
    kernel = (raw - column_mean[None, :]).astype(jnp.bfloat16)
    column_count = targets.shape[1]
    group_width = column_count // GROUPS
    results = [
        conjugate_gradients(
            kernel, targets[:, g * group_width:(g + 1) * group_width], n_rows, sample_bits, landmark_bits
        )
        for g in range(GROUPS)
    ]
    weights = jnp.concatenate([r[0] for r in results], axis=1)
    residual = jnp.concatenate([r[1] for r in results], axis=1)
    return (weights, residual)


def solution(mesh):
    return jax.shard_map(
        on_device,
        mesh=mesh,
        in_specs=(
            P("sample", "landmark"),
            P("sample"),
            P("landmark", None),
            P("landmark"),
            P("landmark"),
            P(),
            P("sample", None),
        ),
        out_specs=(P("landmark", None), P("landmark", None)),
        check_vma=False,
    )
```

```python
import math

import jax
import jax.numpy as jnp
from jax import lax
from jax.sharding import PartitionSpec as P

ITERS = 2
GROUPS = 1


def REDUCE(x, extra, axis, bits, gather_dtype, wire_dtype=jnp.bfloat16):
    return exchange_sum(x, extra, axis, gather_dtype, wire_dtype)


ridge = 0.5


def level_values(level_ids, level_table):
    onehot = level_ids[:, None] == jnp.arange(level_table.shape[0], dtype=jnp.int32)[None, :]
    return jnp.sum(
        jnp.where(onehot, level_table[None, :], jnp.zeros_like(level_table)[None, :]), axis=1
    )


def raw_block(summary_rows, row_factor, anchors, anchor_factor):
    scores = jnp.dot(summary_rows, anchors.T, preferred_element_type=jnp.float32)
    return jnp.exp(scores * row_factor[:, None] * anchor_factor[None, :])


def partner_bits(size, order):
    bits = [b for b in order if b < size]
    assert sorted(bits) == [1 << i for i in range(size.bit_length() - 1)]
    return bits


def butterfly_sum(x, axis, bits):
    size = lax.axis_size(axis)
    for k in bits:
        perm = [(i, i ^ k) for i in range(size)]
        x = x + lax.ppermute(x, axis, perm)
    return x


def pack_rows(extra, columns, wire_dtype):
    rows = extra.reshape(-1, columns)
    if wire_dtype == jnp.float32:
        parts = [rows]
    else:
        parts = []
        rest = rows
        for _ in range(3):
            term = lax.reduce_precision(rest, exponent_bits=8, mantissa_bits=7)
            parts.append(term)
            rest = rest - term
    packed = jnp.concatenate(parts, axis=0).astype(wire_dtype)
    tile = 8 if wire_dtype == jnp.float32 else 16
    return jnp.pad(packed, ((0, -packed.shape[0] % tile), (0, 0)))


def unpack_rows(packed, count, wire_dtype):
    terms = 1 if wire_dtype == jnp.float32 else 3
    packed = packed[: terms * count].astype(jnp.float32).reshape(terms, count, -1)
    total = packed[0]
    for t in range(1, terms):
        total = total + packed[t]
    return total.reshape(-1)


def halving_sum(x, extra, axis, bits, gather_dtype, wire_dtype=jnp.bfloat16):
    size = lax.axis_size(axis)
    index = lax.axis_index(axis)
    columns = x.shape[1]
    for k in bits:
        perm = [(i, i ^ k) for i in range(size)]
        half = x.shape[0] // 2
        mine = (index // k) % 2
        keep = lax.dynamic_slice_in_dim(x, mine * half, half, axis=0)
        send = lax.dynamic_slice_in_dim(x, (1 - mine) * half, half, axis=0).astype(wire_dtype)
        if extra is not None:
            send = jnp.concatenate([send, pack_rows(extra, columns, wire_dtype)], axis=0)
        got = lax.ppermute(send, axis, perm)
        x = keep + got[:half].astype(jnp.float32)
        if extra is not None:
            extra = extra + unpack_rows(got[half:], extra.shape[0] // columns, wire_dtype)
    x = x.astype(gather_dtype)
    for k in reversed(bits):
        perm = [(i, i ^ k) for i in range(size)]
        part = x.shape[0]
        mine = (index // k) % 2
        got = lax.ppermute(x, axis, perm)
        whole = jnp.zeros((2 * part,) + x.shape[1:], x.dtype)
        whole = lax.dynamic_update_slice_in_dim(whole, x, mine * part, axis=0)
        x = lax.dynamic_update_slice_in_dim(whole, got, (1 - mine) * part, axis=0)
    return x, extra


def exchange_scatter(x, extra, axis, wire_dtype):
    size = lax.axis_size(axis)
    rows, columns = x.shape
    chunks = x.reshape(size, rows // size, columns).astype(wire_dtype)
    if extra is not None:
        packed = pack_rows(extra, columns, wire_dtype)
        chunks = jnp.concatenate(
            [chunks, jnp.broadcast_to(packed[None], (size,) + packed.shape)], axis=1
        )
    got = lax.all_to_all(chunks, axis, 0, 0, tiled=False)
    total = jnp.sum(got.astype(jnp.float32), axis=0)
    part = total[: rows // size]
    if extra is not None:
        extra = unpack_rows(total[rows // size:], extra.shape[0] // columns, wire_dtype)
    return part, extra


def exchange_gather(part, axis):
    size = lax.axis_size(axis)
    whole = lax.all_to_all(
        jnp.broadcast_to(part[None], (size,) + part.shape), axis, 0, 0, tiled=False
    )
    return whole.reshape((size * part.shape[0],) + part.shape[1:])


def exchange_sum(x, extra, axis, gather_dtype, wire_dtype=jnp.bfloat16):
    part, extra = exchange_scatter(x, extra, axis, wire_dtype)
    return exchange_gather(part.astype(gather_dtype), axis), extra


def conjugate_gradients(kernel, targets, n_rows, sample_bits, landmark_bits):
    rhs_part = jnp.dot(kernel.T, targets, preferred_element_type=jnp.float32)
    rhs_total, _ = exchange_sum(rhs_part, None, "sample", jnp.float32, jnp.float32)
    rhs = rhs_total / math.sqrt(n_rows)
    column_count = rhs.shape[1]
    weights = jnp.zeros_like(rhs)
    residual = rhs
    direction = rhs
    for iteration in range(ITERS):
        if iteration == 0:
            row_part = jnp.dot(kernel, direction.astype(jnp.bfloat16), preferred_element_type=jnp.float32)
            sums = jnp.concatenate(
                [jnp.sum(direction * direction, axis=0), jnp.sum(residual * residual, axis=0)]
            )
            row_chunk, landmark_sums = exchange_scatter(row_part, sums, "landmark", jnp.bfloat16)
            direction_square = landmark_sums[:column_count]
            norm_now = landmark_sums[column_count:]
        else:
            row_part = jnp.dot(kernel, residual.astype(jnp.bfloat16), preferred_element_type=jnp.float32)
            sums = jnp.concatenate(
                [jnp.sum(residual * residual, axis=0), jnp.sum(residual * direction, axis=0)]
            )
            residual_chunk, landmark_sums = exchange_scatter(row_part, sums, "landmark", jnp.bfloat16)
            norm_next = landmark_sums[:column_count]
            cross = landmark_sums[column_count:]
            beta = norm_next / norm_now
            row_chunk = residual_chunk + beta * row_chunk
            direction = residual + beta * direction
            direction_square = norm_next + 2.0 * beta * cross + beta * beta * direction_square
            norm_now = norm_next
        row_half = exchange_gather(row_chunk.astype(jnp.bfloat16), "landmark")
        row_square = jnp.sum(jnp.square(row_half.astype(jnp.float32)), axis=0)
        column_part = jnp.dot(kernel.T, row_half, preferred_element_type=jnp.float32)
        column_total, row_square_total = exchange_sum(
            column_part, row_square, "sample", jnp.float32, jnp.float32
        )
        image = column_total / n_rows + ridge * direction
        curvature = row_square_total / n_rows + ridge * direction_square
        step_size = norm_now / curvature
        weights = weights + step_size * direction
        residual = residual - step_size * image
    return weights, residual


def on_device(summaries, row_level, pool, pool_level, landmark_index, level_scale, targets):
    sample_bits = partner_bits(lax.axis_size("sample"), (2, 1, 4, 8, 16, 32, 64))
    landmark_bits = partner_bits(lax.axis_size("landmark"), (1, 2, 4, 8, 16, 32, 64))
    row_count = summaries.shape[0]
    n_rows = row_count * lax.axis_size("sample")
    gathered = lax.all_gather(summaries, "landmark", axis=1, tiled=True)
    feature_count = gathered.shape[1]
    anchors = jnp.take(pool, landmark_index, axis=0)
    anchor_level = jnp.take(pool_level, landmark_index, axis=0)
    row_factor = 1.0 / math.sqrt(feature_count) / level_values(row_level, level_scale)
    anchor_factor = 1.0 / level_values(anchor_level, level_scale)
    raw = raw_block(gathered, row_factor, anchors, anchor_factor)
    column_mean = butterfly_sum(jnp.sum(raw, axis=0), "sample", sample_bits) / n_rows
    kernel = (raw - column_mean[None, :]).astype(jnp.bfloat16)
    column_count = targets.shape[1]
    group_width = column_count // GROUPS
    results = [
        conjugate_gradients(
            kernel, targets[:, g * group_width:(g + 1) * group_width], n_rows, sample_bits, landmark_bits
        )
        for g in range(GROUPS)
    ]
    weights = jnp.concatenate([r[0] for r in results], axis=1)
    residual = jnp.concatenate([r[1] for r in results], axis=1)
    return (weights, residual)


def solution(mesh):
    return jax.shard_map(
        on_device,
        mesh=mesh,
        in_specs=(
            P("sample", "landmark"),
            P("sample"),
            P("landmark", None),
            P("landmark"),
            P("landmark"),
            P(),
            P("sample", None),
        ),
        out_specs=(P("landmark", None), P("landmark", None)),
        check_vma=False,
    )
```

```python
import math

import jax
import jax.numpy as jnp
from jax import lax
from jax.sharding import PartitionSpec as P

ITERS = 2
GROUPS = 1


def REDUCE(x, extra, axis, bits, gather_dtype, wire_dtype=jnp.bfloat16):
    return exchange_sum(x, extra, axis, gather_dtype, wire_dtype)


ridge = 0.5


def level_values(level_ids, level_table):
    onehot = level_ids[:, None] == jnp.arange(level_table.shape[0], dtype=jnp.int32)[None, :]
    return jnp.sum(
        jnp.where(onehot, level_table[None, :], jnp.zeros_like(level_table)[None, :]), axis=1
    )


def raw_block(summary_rows, row_factor, anchors, anchor_factor):
    scores = jnp.dot(summary_rows, anchors.T, preferred_element_type=jnp.float32)
    return jnp.exp(scores * row_factor[:, None] * anchor_factor[None, :])


def partner_bits(size, order):
    bits = [b for b in order if b < size]
    assert sorted(bits) == [1 << i for i in range(size.bit_length() - 1)]
    return bits


def butterfly_sum(x, axis, bits):
    size = lax.axis_size(axis)
    for k in bits:
        perm = [(i, i ^ k) for i in range(size)]
        x = x + lax.ppermute(x, axis, perm)
    return x


def pack_rows(extra, columns, wire_dtype):
    rows = extra.reshape(-1, columns)
    if wire_dtype == jnp.float32:
        parts = [rows]
    else:
        parts = []
        rest = rows
        for _ in range(3):
            term = lax.reduce_precision(rest, exponent_bits=8, mantissa_bits=7)
            parts.append(term)
            rest = rest - term
    return jnp.concatenate(parts, axis=0).astype(wire_dtype)


def unpack_rows(packed, count, wire_dtype):
    terms = 1 if wire_dtype == jnp.float32 else 3
    packed = packed.astype(jnp.float32).reshape(terms, count, -1)
    total = packed[0]
    for t in range(1, terms):
        total = total + packed[t]
    return total.reshape(-1)


def halving_sum(x, extra, axis, bits, gather_dtype, wire_dtype=jnp.bfloat16):
    size = lax.axis_size(axis)
    index = lax.axis_index(axis)
    columns = x.shape[1]
    for k in bits:
        perm = [(i, i ^ k) for i in range(size)]
        half = x.shape[0] // 2
        mine = (index // k) % 2
        keep = lax.dynamic_slice_in_dim(x, mine * half, half, axis=0)
        send = lax.dynamic_slice_in_dim(x, (1 - mine) * half, half, axis=0).astype(wire_dtype)
        if extra is not None:
            send = jnp.concatenate([send, pack_rows(extra, columns, wire_dtype)], axis=0)
        got = lax.ppermute(send, axis, perm)
        x = keep + got[:half].astype(jnp.float32)
        if extra is not None:
            extra = extra + unpack_rows(got[half:], extra.shape[0] // columns, wire_dtype)
    x = x.astype(gather_dtype)
    for k in reversed(bits):
        perm = [(i, i ^ k) for i in range(size)]
        part = x.shape[0]
        mine = (index // k) % 2
        got = lax.ppermute(x, axis, perm)
        whole = jnp.zeros((2 * part,) + x.shape[1:], x.dtype)
        whole = lax.dynamic_update_slice_in_dim(whole, x, mine * part, axis=0)
        x = lax.dynamic_update_slice_in_dim(whole, got, (1 - mine) * part, axis=0)
    return x, extra


def exchange_scatter(x, extra, axis, wire_dtype):
    size = lax.axis_size(axis)
    rows, columns = x.shape
    chunks = x.reshape(size, rows // size, columns).astype(wire_dtype)
    if extra is not None:
        packed = pack_rows(extra, columns, wire_dtype)
        chunks = jnp.concatenate(
            [chunks, jnp.broadcast_to(packed[None], (size,) + packed.shape)], axis=1
        )
    got = lax.all_to_all(chunks, axis, 0, 0, tiled=False)
    total = jnp.sum(got.astype(jnp.float32), axis=0)
    part = total[: rows // size]
    if extra is not None:
        extra = unpack_rows(total[rows // size:], extra.shape[0] // columns, wire_dtype)
    return part, extra


def exchange_gather(part, axis):
    size = lax.axis_size(axis)
    whole = lax.all_to_all(
        jnp.broadcast_to(part[None], (size,) + part.shape), axis, 0, 0, tiled=False
    )
    return whole.reshape((size * part.shape[0],) + part.shape[1:])


def exchange_sum(x, extra, axis, gather_dtype, wire_dtype=jnp.bfloat16):
    part, extra = exchange_scatter(x, extra, axis, wire_dtype)
    return exchange_gather(part.astype(gather_dtype), axis), extra


def conjugate_gradients(kernel, targets, n_rows, sample_bits, landmark_bits):
    rhs_part = jnp.dot(kernel.T, targets, preferred_element_type=jnp.float32)
    rhs_total, _ = exchange_sum(rhs_part, None, "sample", jnp.float32, jnp.float32)
    rhs = rhs_total / math.sqrt(n_rows)
    column_count = rhs.shape[1]
    weights = jnp.zeros_like(rhs)
    residual = rhs
    direction = rhs
    for iteration in range(ITERS):
        if iteration == 0:
            row_part = jnp.dot(kernel, direction.astype(jnp.bfloat16), preferred_element_type=jnp.float32)
            sums = jnp.concatenate(
                [jnp.sum(direction * direction, axis=0), jnp.sum(residual * residual, axis=0)]
            )
            row_chunk, landmark_sums = exchange_scatter(row_part, sums, "landmark", jnp.bfloat16)
            direction_square = landmark_sums[:column_count]
            norm_now = landmark_sums[column_count:]
        else:
            row_part = jnp.dot(kernel, residual.astype(jnp.bfloat16), preferred_element_type=jnp.float32)
            sums = jnp.concatenate(
                [jnp.sum(residual * residual, axis=0), jnp.sum(residual * direction, axis=0)]
            )
            residual_chunk, landmark_sums = exchange_scatter(row_part, sums, "landmark", jnp.bfloat16)
            norm_next = landmark_sums[:column_count]
            cross = landmark_sums[column_count:]
            beta = norm_next / norm_now
            row_chunk = residual_chunk + beta * row_chunk
            direction = residual + beta * direction
            direction_square = norm_next + 2.0 * beta * cross + beta * beta * direction_square
            norm_now = norm_next
        row_half = exchange_gather(row_chunk.astype(jnp.bfloat16), "landmark")
        row_square = jnp.sum(jnp.square(row_half.astype(jnp.float32)), axis=0)
        column_part = jnp.dot(kernel.T, row_half, preferred_element_type=jnp.float32)
        column_total, row_square_total = exchange_sum(
            column_part, row_square, "sample", jnp.float32, jnp.float32
        )
        image = column_total / n_rows + ridge * direction
        curvature = row_square_total / n_rows + ridge * direction_square
        step_size = norm_now / curvature
        weights = weights + step_size * direction
        residual = residual - step_size * image
    return weights, residual


def on_device(summaries, row_level, pool, pool_level, landmark_index, level_scale, targets):
    sample_bits = partner_bits(lax.axis_size("sample"), (1, 2, 4, 8, 16, 32, 64))
    landmark_bits = partner_bits(lax.axis_size("landmark"), (1, 2, 4, 8, 16, 32, 64))
    row_count = summaries.shape[0]
    n_rows = row_count * lax.axis_size("sample")
    gathered = lax.all_gather(summaries, "landmark", axis=1, tiled=True)
    feature_count = gathered.shape[1]
    anchors = jnp.take(pool, landmark_index, axis=0)
    anchor_level = jnp.take(pool_level, landmark_index, axis=0)
    row_factor = 1.0 / math.sqrt(feature_count) / level_values(row_level, level_scale)
    anchor_factor = 1.0 / level_values(anchor_level, level_scale)
    raw = raw_block(gathered, row_factor, anchors, anchor_factor)
    column_mean = butterfly_sum(jnp.sum(raw, axis=0), "sample", sample_bits) / n_rows
    kernel = (raw - column_mean[None, :]).astype(jnp.bfloat16)
    column_count = targets.shape[1]
    group_width = column_count // GROUPS
    results = [
        conjugate_gradients(
            kernel, targets[:, g * group_width:(g + 1) * group_width], n_rows, sample_bits, landmark_bits
        )
        for g in range(GROUPS)
    ]
    weights = jnp.concatenate([r[0] for r in results], axis=1)
    residual = jnp.concatenate([r[1] for r in results], axis=1)
    return (weights, residual)


def solution(mesh):
    return jax.shard_map(
        on_device,
        mesh=mesh,
        in_specs=(
            P("sample", "landmark"),
            P("sample"),
            P("landmark", None),
            P("landmark"),
            P("landmark"),
            P(),
            P("sample", None),
        ),
        out_specs=(P("landmark", None), P("landmark", None)),
        check_vma=False,
    )
```
